32 devices in a mesh: starts: 2 (over y), gx: 8 (over z, x), gy: 2 (over core).
Axes of the slice: x: 2, y: 2, z: 4, core: 2. Of those that a mesh axis runs over, the one named last changes fastest.
Arguments:
- chi_final: float32 [2, 64, 128, 256], P(None, ('starts', 'gx'), 'gy'), parts along dimension 1, may hold values from -30 to 30
- psi_late: float32 [2, 64, 128, 256], P(None, ('starts', 'gx'), 'gy'), parts along dimension 1, may hold values from -0.7 to 0.7
- psi_early: float32 [2, 64, 128, 256], P(None, ('starts', 'gx'), 'gy'), parts along dimension 1, may hold values from -0.7 to 0.7
- trap: float32 [32, 128, 256], P('gx', 'gy'), may hold values from 0 to 1
- controls: float32 [4, 64, 256], P('starts', 'gy'), parts along dimension 0, may hold values from -0.5 to 0.5
Outputs:
- chi_start: float32 [2, 64, 128, 256], P(None, ('starts', 'gx'), 'gy'), parts along dimension 1
- grad_rows: float32 [4, 64, 256], P('starts', 'gy'), parts along dimension 0
- adjoint_power: float32 [2], P('starts'), parts along dimension 0
The draws below stay inside these ranges and needn't reach their ends.
There are 2 independent parts, one for each index of `starts`. The reference program is written for one: setup_inputs(seed, part) draws one part's arguments, and reference() takes and returns one part's arrays. A program takes and returns all parts, laid end to end along the dimension named above; an argument that names none is the same for every part. Nothing has to cross between parts.
All inputs are finite; a program needn't handle non-finite values.
Results may differ from the reference program's by a relative error of at most 0.0005.
Values sent between devices are 32-bit elements; how exact they have to be, the bound alone decides.
No kernel may reach another device: no remote copies, remote signals or barrier semaphores. Data moves between devices by JAX's collectives and lax.ppermute only.
A program may use at most 64 MiB of HBM per device.

```python
import math
import jax
import jax.numpy as jnp
from jax import lax

NX = 32
NY = 128
NZ = 256


def draw_chi_final(key, part):
    key_base = jax.random.fold_in(jax.random.fold_in(key, 11), 0)
    base = jnp.clip(jax.random.normal(key_base, (2, NX, NY, NZ), jnp.float32), -5.0, 5.0)
    position = jnp.arange(NX).astype(jnp.float32) / float(max(NX - 1, 1))
    power = (1.0 + 2.0 * position)[:, None, None] * jnp.ones((1, NY, NZ), jnp.float32)
    return base * jnp.sqrt(power)[None]


def steps_of(rng, extent, pieces, least, largest):
    level = 1.0
    for axis_at, shards_of in pieces:
        draws = jax.random.uniform(jax.random.fold_in(jax.random.fold_in(rng, 6), axis_at), (shards_of,), jnp.float32, least / len(pieces), largest / len(pieces))
        level = level * jnp.repeat(jnp.exp(draws), extent[axis_at] // shards_of).reshape((-1,) + (1,) * (len(extent) - 1 - axis_at))
    return level


def setup_inputs(seed: int = 0, part: int = 0) -> dict:
    streams_of = jax.random.split(jax.random.key(seed), 6)
    part_splits = jax.random.split(jax.random.fold_in(streams_of[5], part), 6)
    chi_final = draw_chi_final(jax.random.fold_in(jax.random.fold_in(streams_of[5], part), 71), part)
    psi_late = jnp.clip(jax.random.uniform(part_splits[1], (2, NX, NY, NZ), jnp.float32, -0.7, 0.7) * steps_of(part_splits[1], (2, NX, NY, NZ), ((1, 8), (2, 2)), -0.4, 0.0), -0.7, 0.7)
    psi_early = jnp.clip(jax.random.uniform(part_splits[2], (2, NX, NY, NZ), jnp.float32, -0.7, 0.7) * steps_of(part_splits[2], (2, NX, NY, NZ), ((1, 8), (2, 2)), -0.4, 0.0), -0.7, 0.7)
    trap = jnp.clip(1.0 * jax.random.uniform(streams_of[3], (NX, NY, NZ), jnp.float32) ** steps_of(streams_of[3], (NX, NY, NZ), ((0, 8), (1, 2)), -0.2, 0.2), 0.0, 1.0)
    controls = jnp.clip(jax.random.uniform(part_splits[4], (2, NY // 2, NZ), jnp.float32, -0.5, 0.5) * steps_of(part_splits[4], (2, NY // 2, NZ), ((1, 2),), -0.4, 0.0), -0.5, 0.5)
    return dict(chi_final=chi_final, psi_late=psi_late, psi_early=psi_early, trap=trap, controls=controls)


COUPLING = 1.0
STEP_SIZE = 0.2

def profile_of(x_index, total):
    return 1.0 + 0.5 * jnp.cos(2.0 * math.pi * x_index / total)

def coefficients(psi, trap, control, profile):
    real_part = psi[0]
    imag_part = psi[1]
    fine_control = jnp.repeat(control, 2, axis=0)
    potential = trap + profile[:, None, None] * fine_control[None, :, :]
    weight = potential + 2.0 * COUPLING * (real_part * real_part + imag_part * imag_part)
    mix_a = COUPLING * (real_part * real_part - imag_part * imag_part)
    mix_b = 2.0 * COUPLING * real_part * imag_part
    return (weight, mix_a, mix_b)

def laplace(field):
    padded = jnp.pad(field, ((0, 0), (1, 1), (1, 1), (1, 1)))
    total = padded[:, 2:, 1:-1, 1:-1] + padded[:, :-2, 1:-1, 1:-1]
    total = total + padded[:, 1:-1, 2:, 1:-1] + padded[:, 1:-1, :-2, 1:-1]
    total = total + padded[:, 1:-1, 1:-1, 2:] + padded[:, 1:-1, 1:-1, :-2]
    return total - 6.0 * field

def operator(field, coef):
    weight, mix_a, mix_b = coef
    lapl = laplace(field)
    real_part = field[0]
    imag_part = field[1]
    upper = -0.5 * lapl[0] + (weight + mix_a) * real_part + mix_b * imag_part
    lower = -0.5 * lapl[1] + mix_b * real_part + (weight - mix_a) * imag_part
    return jnp.stack([-lower, upper])

def rk_step(field, coef):
    section_one = operator(field, coef)
    section_two = operator(field + 0.5 * STEP_SIZE * section_one, coef)
    section_three = operator(field + 0.5 * STEP_SIZE * section_two, coef)
    section_four = operator(field + STEP_SIZE * section_three, coef)
    return field + STEP_SIZE / 6.0 * (section_one + 2.0 * section_two + 2.0 * section_three + section_four)

def row_terms(field, psi, profile):
    intersection = field[0] * psi[1] - field[1] * psi[0]
    summed = lax.optimization_barrier(jnp.sum(intersection * profile[:, None, None], axis=0))
    return summed.reshape(summed.shape[0] // 2, 2, summed.shape[1]).sum(axis=1)

def reference(chi_final, psi_late, psi_early, trap, controls):
    profile = profile_of(jnp.arange(NX).astype(jnp.float32), float(NX))
    chi_late = rk_step(chi_final, coefficients(psi_late, trap, controls[1], profile))
    chi_start = rk_step(chi_late, coefficients(psi_early, trap, controls[0], profile))
    rows = jnp.stack([row_terms(chi_start, psi_early, profile), row_terms(chi_late, psi_late, profile)])
    power = jnp.sum(chi_start * chi_start) / float(NX * NY * NZ)
    grad_rows = rows / jnp.sqrt(float(NX) * (power + 1e-06))
    return (chi_start, grad_rows, jnp.reshape(power, (1,)).astype(jnp.float32))
```

```python
import math

import jax
import jax.numpy as jnp
from jax import lax
from jax.sharding import PartitionSpec as P

COUPLING = 1.0
STEP_SIZE = 0.2


def halo(block, axis, dim, width):
    count = lax.axis_size(axis)
    forward = [(i, i + 1) for i in range(count - 1)]
    backward = [(target, source) for source, target in forward]
    low = lax.ppermute(
        lax.slice_in_dim(block, block.shape[dim] - width, None, axis=dim), axis, forward
    )
    high = lax.ppermute(lax.slice_in_dim(block, 0, width, axis=dim), axis, backward)
    return low, high


def axis_sum(value, axis):
    count = lax.axis_size(axis)
    if count & (count - 1):
        return lax.psum(value, axis)
    step = 1
    while step < count:
        pairs = [(i, i ^ step) for i in range(count)]
        value = value + lax.ppermute(value, axis, pairs)
        step *= 2
    return value


def coefficients(psi, trap, control, profile):
    real_part = psi[0]
    imag_part = psi[1]
    fine_control = jnp.repeat(control, 2, axis=0)
    potential = trap + profile[:, None, None] * fine_control[None, :, :]
    weight = potential + 2.0 * COUPLING * (real_part * real_part + imag_part * imag_part)
    mix_a = COUPLING * (real_part * real_part - imag_part * imag_part)
    mix_b = 2.0 * COUPLING * real_part * imag_part
    return (weight, mix_a, mix_b)


def apply_coef(lapl, field, coef):
    weight, mix_a, mix_b = coef
    real_part = field[0]
    imag_part = field[1]
    upper = -0.5 * lapl[0] + (weight + mix_a) * real_part + mix_b * imag_part
    lower = -0.5 * lapl[1] + mix_b * real_part + (weight - mix_a) * imag_part
    return jnp.stack([-lower, upper])


def operator(field, coef):
    x_low, x_high = halo(field, "gx", 1, 1)
    y_low, y_high = halo(field, "gy", 2, 1)
    x_padded = jnp.concatenate([x_low, field, x_high], axis=1)
    y_padded = jnp.concatenate([y_low, field, y_high], axis=2)
    z_padded = jnp.pad(field, ((0, 0), (0, 0), (0, 0), (1, 1)))
    total = x_padded[:, 2:] + x_padded[:, :-2]
    total = total + y_padded[:, :, 2:] + y_padded[:, :, :-2]
    total = total + z_padded[:, :, :, 2:] + z_padded[:, :, :, :-2]
    lapl = total - 6.0 * field
    return apply_coef(lapl, field, coef)


def rk_step(field, coef):
    section_one = operator(field, coef)
    section_two = operator(field + 0.5 * STEP_SIZE * section_one, coef)
    section_three = operator(field + 0.5 * STEP_SIZE * section_two, coef)
    section_four = operator(field + STEP_SIZE * section_three, coef)
    return field + STEP_SIZE / 6.0 * (
        section_one + 2.0 * section_two + 2.0 * section_three + section_four
    )


def row_terms(field, psi, profile):
    intersection = field[0] * psi[1] - field[1] * psi[0]
    summed = jnp.sum(intersection * profile[:, None, None], axis=0)
    return summed.reshape(summed.shape[0] // 2, 2, summed.shape[1]).sum(axis=1)


def on_device(chi_final, psi_late, psi_early, trap, controls):
    planes = chi_final.shape[1]
    width_y = chi_final.shape[2]
    depth = chi_final.shape[3]
    total_x = planes * lax.axis_size("gx")
    total_y = width_y * lax.axis_size("gy")
    first = lax.axis_index("gx") * planes
    x_index = (first + jnp.arange(planes, dtype=jnp.int32)).astype(jnp.float32)
    profile = 1.0 + 0.5 * jnp.cos(2.0 * math.pi * x_index / float(total_x))
    coef_late = coefficients(psi_late, trap, controls[1], profile)
    coef_early = coefficients(psi_early, trap, controls[0], profile)
    chi_late = rk_step(chi_final, coef_late)
    rows_late = axis_sum(row_terms(chi_late, psi_late, profile), "gx")
    chi_start = rk_step(chi_late, coef_early)
    rows_early = row_terms(chi_start, psi_early, profile)
    local_sq = jnp.sum(chi_start * chi_start)
    extra = jnp.zeros((1, rows_early.shape[1]), jnp.float32).at[0, 0].set(local_sq)
    packed = axis_sum(jnp.concatenate([rows_early, extra], axis=0), "gx")
    squares = axis_sum(packed[-1, 0], "gy")
    rows_sum = jnp.stack([packed[:-1], rows_late])
    power = squares / float(total_x * total_y * depth)
    grad_rows = rows_sum / jnp.sqrt(float(total_x) * (power + 1e-06))
    return (chi_start, grad_rows, jnp.reshape(power, (1,)))


def solution(mesh):
    placed = (
        P(None, ("starts", "gx"), "gy", None),
        P(None, ("starts", "gx"), "gy", None),
        P(None, ("starts", "gx"), "gy", None),
        P("gx", "gy", None),
        P("starts", "gy", None),
    )
    return jax.shard_map(
        on_device,
        mesh=mesh,
        in_specs=placed,
        out_specs=(P(None, ("starts", "gx"), "gy", None), P("starts", "gy", None), P("starts")),
        check_vma=False,
    )
```

```python
import math

import jax
import jax.numpy as jnp
from jax import lax
from jax.sharding import PartitionSpec as P

COUPLING = 1.0
STEP_SIZE = 0.2
DEPTH = 4


def axis_sum(value, axis):
    count = lax.axis_size(axis)
    if count & (count - 1):
        return lax.psum(value, axis)
    step = 1
    while step < count:
        pairs = [(i, i ^ step) for i in range(count)]
        value = value + lax.ppermute(value, axis, pairs)
        step *= 2
    return value


def swap_y(value):
    return lax.ppermute(value, "gy", [(0, 1), (1, 0)])


def extend(block, w):
    nx = lax.axis_size("gx")
    ny = lax.axis_size("gy")
    iy = lax.axis_index("gy")
    X, Y = block.shape[1], block.shape[2]
    up = [(i, i + 1) for i in range(nx - 1)]
    down = [(i + 1, i) for i in range(nx - 1)]
    x_low = lax.ppermute(block[:, X - w:], "gx", up)
    x_high = lax.ppermute(block[:, :w], "gx", down)
    strip = lax.dynamic_slice_in_dim(block, (1 - iy) * (Y - w), w, axis=2)
    y_other = swap_y(strip)
    up_d = [(i * ny + j, (i + 1) * ny + (1 - j)) for i in range(nx - 1) for j in range(ny)]
    down_d = [((i + 1) * ny + j, i * ny + (1 - j)) for i in range(nx - 1) for j in range(ny)]
    c_low = lax.ppermute(strip[:, X - w:], ("gx", "gy"), up_d)
    c_high = lax.ppermute(strip[:, :w], ("gx", "gy"), down_d)
    main = jnp.concatenate([x_low, block, x_high], axis=1)
    side = jnp.concatenate([c_low, y_other, c_high], axis=1)
    zero = jnp.zeros_like(side)
    below = jnp.where(iy == 1, side, zero)
    above = jnp.where(iy == 0, side, zero)
    return jnp.concatenate([below, main, above], axis=2)


def crop(a, k):
    if k == 0:
        return a
    return a[..., k:a.shape[-3] - k, k:a.shape[-2] - k, :]


def coefficients(psi, trap, fine_control, profile):
    real_part = psi[0]
    imag_part = psi[1]
    potential = trap + profile[:, None, None] * fine_control[None, :, :]
    weight = potential + 2.0 * COUPLING * (real_part * real_part + imag_part * imag_part)
    mix_a = COUPLING * (real_part * real_part - imag_part * imag_part)
    mix_b = 2.0 * COUPLING * real_part * imag_part
    return (weight, mix_a, mix_b)


def apply_coef(lapl, field, coef):
    weight, mix_a, mix_b = coef
    real_part = field[0]
    imag_part = field[1]
    upper = -0.5 * lapl[0] + (weight + mix_a) * real_part + mix_b * imag_part
    lower = -0.5 * lapl[1] + mix_b * real_part + (weight - mix_a) * imag_part
    return jnp.stack([-lower, upper])


def operator(field, coef):
    center = crop(field, 1)
    z_padded = jnp.pad(center, ((0, 0), (0, 0), (0, 0), (1, 1)))
    total = field[:, 2:, 1:-1] + field[:, :-2, 1:-1]
    total = total + field[:, 1:-1, 2:] + field[:, 1:-1, :-2]
    total = total + z_padded[:, :, :, 2:] + z_padded[:, :, :, :-2]
    lapl = total - 6.0 * center
    return apply_coef(lapl, center, coef)


def rk_step(field, coef, inside):
    def masked(value, k):
        return jnp.where(crop(inside, k), value, 0.0)

    def cut(coef_k, k):
        return tuple(crop(c, k) for c in coef_k)

    section_one = operator(field, coef)
    stage_two = masked(crop(field, 1) + 0.5 * STEP_SIZE * section_one, 1)
    section_two = operator(stage_two, cut(coef, 1))
    stage_three = masked(crop(field, 2) + 0.5 * STEP_SIZE * section_two, 2)
    section_three = operator(stage_three, cut(coef, 2))
    stage_four = masked(crop(field, 3) + STEP_SIZE * section_three, 3)
    section_four = operator(stage_four, cut(coef, 3))
    return crop(field, 4) + STEP_SIZE / 6.0 * (
        crop(section_one, 3) + 2.0 * crop(section_two, 2) + 2.0 * crop(section_three, 1)
        + section_four
    )


def row_terms(field, psi, profile):
    intersection = field[0] * psi[1] - field[1] * psi[0]
    summed = jnp.sum(intersection * profile[:, None, None], axis=0)
    return summed.reshape(summed.shape[0] // 2, 2, summed.shape[1]).sum(axis=1)


def on_device(chi_final, psi_late, psi_early, trap, controls):
    w = DEPTH
    planes = chi_final.shape[1]
    width_y = chi_final.shape[2]
    depth = chi_final.shape[3]
    total_x = planes * lax.axis_size("gx")
    total_y = width_y * lax.axis_size("gy")
    ix = lax.axis_index("gx")
    iy = lax.axis_index("gy")

    late_ext = extend(jnp.concatenate([chi_final, psi_late, trap[None]], axis=0), w)
    early_ext = extend(psi_early, w)
    other_controls = swap_y(controls)
    all_controls = jnp.where(
        iy == 0,
        jnp.concatenate([controls, other_controls], axis=1),
        jnp.concatenate([other_controls, controls], axis=1),
    )
    fine = jnp.repeat(all_controls, 2, axis=1)
    fine = jnp.pad(fine, ((0, 0), (w, w), (0, 0)))
    fine = lax.dynamic_slice_in_dim(fine, iy * width_y + 1, width_y + 2 * w - 2, axis=1)

    x_global = ix * planes - w + jnp.arange(planes + 2 * w, dtype=jnp.int32)
    y_global = iy * width_y - w + jnp.arange(width_y + 2 * w, dtype=jnp.int32)
    inside = ((x_global >= 0) & (x_global < total_x))[:, None, None] & (
        (y_global >= 0) & (y_global < total_y)
    )[None, :, None]
    profile_ext = 1.0 + 0.5 * jnp.cos(2.0 * math.pi * x_global.astype(jnp.float32) / float(total_x))
    profile = profile_ext[w:w + planes]
    profile_3 = profile_ext[1:-1]

    coef_late = coefficients(crop(late_ext[2:4], 1), crop(late_ext[4], 1), fine[1], profile_3)
    coef_early = coefficients(crop(early_ext, 1), crop(late_ext[4], 1), fine[0], profile_3)

    chi_late = rk_step(late_ext[0:2], coef_late, inside)
    chi_start = rk_step(extend(chi_late, w), coef_early, inside)

    rows_late = row_terms(chi_late, psi_late, profile)
    rows_early = row_terms(chi_start, psi_early, profile)
    local_sq = jnp.sum(chi_start * chi_start)
    extra = jnp.zeros((1, rows_early.shape[1]), jnp.float32).at[0, 0].set(local_sq)
    packed = axis_sum(jnp.concatenate([rows_early, rows_late, extra], axis=0), "gx")
    squares = axis_sum(packed[-1, 0], "gy")
    half = rows_early.shape[0]
    rows_sum = jnp.stack([packed[:half], packed[half:2 * half]])
    power = squares / float(total_x * total_y * depth)
    grad_rows = rows_sum / jnp.sqrt(float(total_x) * (power + 1e-06))
    return (chi_start, grad_rows, jnp.reshape(power, (1,)))


def solution(mesh):
    placed = (
        P(None, ("starts", "gx"), "gy", None),
        P(None, ("starts", "gx"), "gy", None),
        P(None, ("starts", "gx"), "gy", None),
        P("gx", "gy", None),
        P("starts", "gy", None),
    )
    return jax.shard_map(
        on_device,
        mesh=mesh,
        in_specs=placed,
        out_specs=(P(None, ("starts", "gx"), "gy", None), P("starts", "gy", None), P("starts")),
        check_vma=False,
    )
```

```python
import math

import jax
import jax.numpy as jnp
from jax import lax
from jax.sharding import PartitionSpec as P

COUPLING = 1.0
STEP_SIZE = 0.2
DEPTH = 2


def axis_sum(value, axis):
    count = lax.axis_size(axis)
    if count & (count - 1):
        return lax.psum(value, axis)
    step = 1
    while step < count:
        pairs = [(i, i ^ step) for i in range(count)]
        value = value + lax.ppermute(value, axis, pairs)
        step *= 2
    return value


def swap_y(value):
    return lax.ppermute(value, "gy", [(0, 1), (1, 0)])


def extend(block, w):
    nx = lax.axis_size("gx")
    ny = lax.axis_size("gy")
    iy = lax.axis_index("gy")
    X, Y = block.shape[1], block.shape[2]
    if ny == 2:
        strip = lax.dynamic_slice_in_dim(block, (1 - iy) * (Y - w), w, axis=2)
        other = swap_y(strip)
        zero = jnp.zeros_like(other)
        below = jnp.where(iy == 1, other, zero)
        above = jnp.where(iy == 0, other, zero)
    else:
        below = lax.ppermute(block[:, :, Y - w:], "gy", [(j, j + 1) for j in range(ny - 1)])
        above = lax.ppermute(block[:, :, :w], "gy", [(j + 1, j) for j in range(ny - 1)])
    up = [(i, i + 1) for i in range(nx - 1)]
    down = [(i + 1, i) for i in range(nx - 1)]
    if w == 1:
        x_low = lax.ppermute(block[:, X - w:], "gx", up)
        x_high = lax.ppermute(block[:, :w], "gx", down)
        corner = jnp.zeros(x_low.shape[:2] + (w,) + x_low.shape[3:], block.dtype)
        x_low = jnp.concatenate([corner, x_low, corner], axis=2)
        x_high = jnp.concatenate([corner, x_high, corner], axis=2)
        tall = jnp.concatenate([below, block, above], axis=2)
    else:
        tall = jnp.concatenate([below, block, above], axis=2)
        x_low = lax.ppermute(tall[:, X - w:], "gx", up)
        x_high = lax.ppermute(tall[:, :w], "gx", down)
    return jnp.concatenate([x_low, tall, x_high], axis=1)


def crop(a, k):
    if k == 0:
        return a
    return a[..., k:a.shape[-3] - k, k:a.shape[-2] - k, :]


def coefficients(psi, trap, fine_control, profile):
    real_part = psi[0]
    imag_part = psi[1]
    potential = trap + profile[:, None, None] * fine_control[None, :, :]
    weight = potential + 2.0 * COUPLING * (real_part * real_part + imag_part * imag_part)
    mix_a = COUPLING * (real_part * real_part - imag_part * imag_part)
    mix_b = 2.0 * COUPLING * real_part * imag_part
    return (weight, mix_a, mix_b)


def apply_coef(lapl, field, coef):
    weight, mix_a, mix_b = coef
    real_part = field[0]
    imag_part = field[1]
    upper = -0.5 * lapl[0] + (weight + mix_a) * real_part + mix_b * imag_part
    lower = -0.5 * lapl[1] + mix_b * real_part + (weight - mix_a) * imag_part
    return jnp.stack([-lower, upper])


def operator(field, coef):
    center = crop(field, 1)
    z_padded = jnp.pad(center, ((0, 0), (0, 0), (0, 0), (1, 1)))
    total = field[:, 2:, 1:-1] + field[:, :-2, 1:-1]
    total = total + field[:, 1:-1, 2:] + field[:, 1:-1, :-2]
    total = total + z_padded[:, :, :, 2:] + z_padded[:, :, :, :-2]
    lapl = total - 6.0 * center
    return apply_coef(lapl, center, coef)


def rk_step(field, coef, inside, w):
    weights = (0.5 * STEP_SIZE, 0.5 * STEP_SIZE, STEP_SIZE)
    sections = []
    stage, reach = field, w
    for k in range(4):
        if reach == 0:
            stage, reach = extend(stage, w), w
        section = operator(stage, tuple(crop(c, w - reach) for c in coef))
        reach -= 1
        sections.append(crop(section, reach))
        if k < 3:
            stage = crop(field, w - reach) + weights[k] * section
            stage = jnp.where(crop(inside, w - reach), stage, 0.0)
    section_one, section_two, section_three, section_four = sections
    return crop(field, w) + STEP_SIZE / 6.0 * (
        section_one + 2.0 * section_two + 2.0 * section_three + section_four
    )


def row_terms(field, psi, profile):
    intersection = field[0] * psi[1] - field[1] * psi[0]
    summed = jnp.sum(intersection * profile[:, None, None], axis=0)
    return summed.reshape(summed.shape[0] // 2, 2, summed.shape[1]).sum(axis=1)


def on_device(chi_final, psi_late, psi_early, trap, controls):
    w = DEPTH
    planes = chi_final.shape[1]
    width_y = chi_final.shape[2]
    depth = chi_final.shape[3]
    total_x = planes * lax.axis_size("gx")
    total_y = width_y * lax.axis_size("gy")
    ix = lax.axis_index("gx")
    iy = lax.axis_index("gy")

    cd = w - 1
    sources = jnp.concatenate([psi_late, psi_early, trap[None]], axis=0)
    if cd > 0:
        sources = extend(sources, cd)
        other_controls = swap_y(controls)
        all_controls = jnp.where(
            iy == 0,
            jnp.concatenate([controls, other_controls], axis=1),
            jnp.concatenate([other_controls, controls], axis=1),
        )
        fine = jnp.repeat(all_controls, 2, axis=1)
        fine = jnp.pad(fine, ((0, 0), (cd, cd), (0, 0)))
        fine = lax.dynamic_slice_in_dim(fine, iy * width_y, width_y + 2 * cd, axis=1)
    else:
        fine = jnp.repeat(controls, 2, axis=1)
    chi_ext = extend(chi_final, w)

    x_global = ix * planes - w + jnp.arange(planes + 2 * w, dtype=jnp.int32)
    y_global = iy * width_y - w + jnp.arange(width_y + 2 * w, dtype=jnp.int32)
    inside = ((x_global >= 0) & (x_global < total_x))[:, None, None] & (
        (y_global >= 0) & (y_global < total_y)
    )[None, :, None]
    profile_ext = 1.0 + 0.5 * jnp.cos(2.0 * math.pi * x_global.astype(jnp.float32) / float(total_x))
    profile = profile_ext[w:w + planes]
    profile_c = profile_ext[1:-1]

    coef_late = coefficients(sources[0:2], sources[4], fine[1], profile_c)
    coef_early = coefficients(sources[2:4], sources[4], fine[0], profile_c)

    chi_late = rk_step(chi_ext, coef_late, inside, w)
    chi_start = rk_step(extend(chi_late, w), coef_early, inside, w)

    rows_late = row_terms(chi_late, psi_late, profile)
    rows_early = row_terms(chi_start, psi_early, profile)
    local_sq = jnp.sum(chi_start * chi_start)
    extra = jnp.zeros((1, rows_early.shape[1]), jnp.float32).at[0, 0].set(local_sq)
    packed = axis_sum(jnp.concatenate([rows_early, rows_late, extra], axis=0), "gx")
    squares = axis_sum(packed[-1, 0], "gy")
    half = rows_early.shape[0]
    rows_sum = jnp.stack([packed[:half], packed[half:2 * half]])
    power = squares / float(total_x * total_y * depth)
    grad_rows = rows_sum / jnp.sqrt(float(total_x) * (power + 1e-06))
    return (chi_start, grad_rows, jnp.reshape(power, (1,)))


def solution(mesh):
    placed = (
        P(None, ("starts", "gx"), "gy", None),
        P(None, ("starts", "gx"), "gy", None),
        P(None, ("starts", "gx"), "gy", None),
        P("gx", "gy", None),
        P("starts", "gy", None),
    )
    return jax.shard_map(
        on_device,
        mesh=mesh,
        in_specs=placed,
        out_specs=(P(None, ("starts", "gx"), "gy", None), P("starts", "gy", None), P("starts")),
        check_vma=False,
    )
```

```python
import math

import jax
import jax.numpy as jnp
from jax import lax
from jax.sharding import PartitionSpec as P

COUPLING = 1.0
STEP_SIZE = 0.2
DEPTH = 2


def axis_sum(value, axis):
    count = lax.axis_size(axis)
    if count & (count - 1):
        return lax.psum(value, axis)
    step = 1
    while step < count:
        pairs = [(i, i ^ step) for i in range(count)]
        value = value + lax.ppermute(value, axis, pairs)
        step *= 2
    return value


def send(value, axis, pairs):
    flat = value.reshape(-1, value.shape[-1])
    return lax.ppermute(flat, axis, pairs).reshape(value.shape)


def swap_y(value):
    return send(value, "gy", [(0, 1), (1, 0)])


def extend(block, w):
    nx = lax.axis_size("gx")
    ny = lax.axis_size("gy")
    iy = lax.axis_index("gy")
    X, Y = block.shape[1], block.shape[2]
    if ny == 2:
        strip = lax.dynamic_slice_in_dim(block, (1 - iy) * (Y - w), w, axis=2)
        other = swap_y(strip)
        zero = jnp.zeros_like(other)
        below = jnp.where(iy == 1, other, zero)
        above = jnp.where(iy == 0, other, zero)
    else:
        below = send(block[:, :, Y - w:], "gy", [(j, j + 1) for j in range(ny - 1)])
        above = send(block[:, :, :w], "gy", [(j + 1, j) for j in range(ny - 1)])
    up = [(i, i + 1) for i in range(nx - 1)]
    down = [(i + 1, i) for i in range(nx - 1)]
    if w == 1:
        x_low = send(block[:, X - w:], "gx", up)
        x_high = send(block[:, :w], "gx", down)
        corner = jnp.zeros(x_low.shape[:2] + (w,) + x_low.shape[3:], block.dtype)
        x_low = jnp.concatenate([corner, x_low, corner], axis=2)
        x_high = jnp.concatenate([corner, x_high, corner], axis=2)
        tall = jnp.concatenate([below, block, above], axis=2)
    else:
        tall = jnp.concatenate([below, block, above], axis=2)
        x_low = send(tall[:, X - w:], "gx", up)
        x_high = send(tall[:, :w], "gx", down)
    return jnp.concatenate([x_low, tall, x_high], axis=1)


def crop(a, k):
    if k == 0:
        return a
    return a[..., k:a.shape[-3] - k, k:a.shape[-2] - k, :]


def coefficients(psi, trap, fine_control, profile):
    real_part = psi[0]
    imag_part = psi[1]
    potential = trap + profile[:, None, None] * fine_control[None, :, :]
    weight = potential + 2.0 * COUPLING * (real_part * real_part + imag_part * imag_part)
    mix_a = COUPLING * (real_part * real_part - imag_part * imag_part)
    mix_b = 2.0 * COUPLING * real_part * imag_part
    return (weight, mix_a, mix_b)


def apply_coef(lapl, field, coef):
    weight, mix_a, mix_b = coef
    real_part = field[0]
    imag_part = field[1]
    upper = -0.5 * lapl[0] + (weight + mix_a) * real_part + mix_b * imag_part
    lower = -0.5 * lapl[1] + mix_b * real_part + (weight - mix_a) * imag_part
    return jnp.stack([-lower, upper])


def operator(field, coef):
    center = crop(field, 1)
    z_padded = jnp.pad(center, ((0, 0), (0, 0), (0, 0), (1, 1)))
    total = field[:, 2:, 1:-1] + field[:, :-2, 1:-1]
    total = total + field[:, 1:-1, 2:] + field[:, 1:-1, :-2]
    total = total + z_padded[:, :, :, 2:] + z_padded[:, :, :, :-2]
    lapl = total - 6.0 * center
    return apply_coef(lapl, center, coef)


def rk_step(field, coef, inside, w):
    weights = (0.5 * STEP_SIZE, 0.5 * STEP_SIZE, STEP_SIZE)
    sections = []
    stage, reach = field, w
    for k in range(4):
        if reach == 0:
            stage, reach = extend(stage, w), w
        section = operator(stage, tuple(crop(c, w - reach) for c in coef))
        reach -= 1
        sections.append(crop(section, reach))
        if k < 3:
            stage = crop(field, w - reach) + weights[k] * section
            stage = jnp.where(crop(inside, w - reach), stage, 0.0)
    section_one, section_two, section_three, section_four = sections
    return crop(field, w) + STEP_SIZE / 6.0 * (
        section_one + 2.0 * section_two + 2.0 * section_three + section_four
    )


def row_terms(field, psi, profile):
    intersection = field[0] * psi[1] - field[1] * psi[0]
    summed = jnp.sum(intersection * profile[:, None, None], axis=0)
    return summed.reshape(summed.shape[0] // 2, 2, summed.shape[1]).sum(axis=1)


def on_device(chi_final, psi_late, psi_early, trap, controls):
    w = DEPTH
    planes = chi_final.shape[1]
    width_y = chi_final.shape[2]
    depth = chi_final.shape[3]
    total_x = planes * lax.axis_size("gx")
    total_y = width_y * lax.axis_size("gy")
    ix = lax.axis_index("gx")
    iy = lax.axis_index("gy")

    cd = w - 1
    sources = jnp.concatenate([psi_late, psi_early, trap[None]], axis=0)
    if cd > 0:
        sources = extend(sources, cd)
        other_controls = swap_y(controls)
        all_controls = jnp.where(
            iy == 0,
            jnp.concatenate([controls, other_controls], axis=1),
            jnp.concatenate([other_controls, controls], axis=1),
        )
        fine = jnp.repeat(all_controls, 2, axis=1)
        fine = jnp.pad(fine, ((0, 0), (cd, cd), (0, 0)))
        fine = lax.dynamic_slice_in_dim(fine, iy * width_y, width_y + 2 * cd, axis=1)
    else:
        fine = jnp.repeat(controls, 2, axis=1)
    chi_ext = extend(chi_final, w)

    x_global = ix * planes - w + jnp.arange(planes + 2 * w, dtype=jnp.int32)
    y_global = iy * width_y - w + jnp.arange(width_y + 2 * w, dtype=jnp.int32)
    inside = ((x_global >= 0) & (x_global < total_x))[:, None, None] & (
        (y_global >= 0) & (y_global < total_y)
    )[None, :, None]
    profile_ext = 1.0 + 0.5 * jnp.cos(2.0 * math.pi * x_global.astype(jnp.float32) / float(total_x))
    profile = profile_ext[w:w + planes]
    profile_c = profile_ext[1:-1]

    coef_late = coefficients(sources[0:2], sources[4], fine[1], profile_c)
    coef_early = coefficients(sources[2:4], sources[4], fine[0], profile_c)

    chi_late = rk_step(chi_ext, coef_late, inside, w)
    chi_start = rk_step(extend(chi_late, w), coef_early, inside, w)

    rows_late = row_terms(chi_late, psi_late, profile)
    rows_early = row_terms(chi_start, psi_early, profile)
    local_sq = jnp.sum(chi_start * chi_start)
    extra = jnp.zeros((1, rows_early.shape[1]), jnp.float32).at[0, 0].set(local_sq)
    packed = axis_sum(jnp.concatenate([rows_early, rows_late, extra], axis=0), "gx")
    squares = axis_sum(packed[-1, 0], "gy")
    half = rows_early.shape[0]
    rows_sum = jnp.stack([packed[:half], packed[half:2 * half]])
    power = squares / float(total_x * total_y * depth)
    grad_rows = rows_sum / jnp.sqrt(float(total_x) * (power + 1e-06))
    return (chi_start, grad_rows, jnp.reshape(power, (1,)))


def solution(mesh):
    placed = (
        P(None, ("starts", "gx"), "gy", None),
        P(None, ("starts", "gx"), "gy", None),
        P(None, ("starts", "gx"), "gy", None),
        P("gx", "gy", None),
        P("starts", "gy", None),
    )
    return jax.shard_map(
        on_device,
        mesh=mesh,
        in_specs=placed,
        out_specs=(P(None, ("starts", "gx"), "gy", None), P("starts", "gy", None), P("starts")),
        check_vma=False,
    )
```

```python
import math

import jax
import jax.numpy as jnp
from jax import lax
from jax.sharding import PartitionSpec as P

COUPLING = 1.0
STEP_SIZE = 0.2


def axis_sum(value, axis):
    count = lax.axis_size(axis)
    if count & (count - 1):
        return lax.psum(value, axis)
    step = 1
    while step < count:
        pairs = [(i, i ^ step) for i in range(count)]
        value = value + lax.ppermute(value, axis, pairs)
        step *= 2
    return value


def y_extended(block):
    ny = lax.axis_size("gy")
    iy = lax.axis_index("gy")
    Y = block.shape[2]
    if ny == 2:
        strip = lax.dynamic_slice_in_dim(block, (1 - iy) * (Y - 1), 1, axis=2)
        other = lax.ppermute(strip, "gy", [(0, 1), (1, 0)])
        zero = jnp.zeros_like(other)
        below = jnp.where(iy == 1, other, zero)
        above = jnp.where(iy == 0, other, zero)
    else:
        below = lax.ppermute(block[:, :, Y - 1:], "gy", [(j, j + 1) for j in range(ny - 1)])
        above = lax.ppermute(block[:, :, :1], "gy", [(j + 1, j) for j in range(ny - 1)])
    return jnp.concatenate([below, block, above], axis=2)


def coefficients(psi, trap, control, profile):
    real_part = psi[0]
    imag_part = psi[1]
    fine_control = jnp.repeat(control, 2, axis=0)
    potential = trap + profile[:, None, None] * fine_control[None, :, :]
    weight = potential + 2.0 * COUPLING * (real_part * real_part + imag_part * imag_part)
    mix_a = COUPLING * (real_part * real_part - imag_part * imag_part)
    mix_b = 2.0 * COUPLING * real_part * imag_part
    return (weight, mix_a, mix_b)


def apply_coef(lapl, field, coef):
    weight, mix_a, mix_b = coef
    real_part = field[0]
    imag_part = field[1]
    upper = -0.5 * lapl[0] + (weight + mix_a) * real_part + mix_b * imag_part
    lower = -0.5 * lapl[1] + mix_b * real_part + (weight - mix_a) * imag_part
    return jnp.stack([-lower, upper])


def operator(tall, x_low, x_high, coef):
    field = tall[:, :, 1:-1]
    x_padded = jnp.concatenate([x_low, field, x_high], axis=1)
    z_padded = jnp.pad(field, ((0, 0), (0, 0), (0, 0), (1, 1)))
    total = x_padded[:, 2:] + x_padded[:, :-2]
    total = total + tall[:, :, 2:] + tall[:, :, :-2]
    total = total + z_padded[:, :, :, 2:] + z_padded[:, :, :, :-2]
    lapl = total - 6.0 * field
    return apply_coef(lapl, field, coef)


def cut(coef, lo, hi):
    return tuple(c[lo:hi] for c in coef)


def across(plane):
    return jnp.stack([0.5 * plane[1], -0.5 * plane[0]])


def stage_pair(stage, base, base_low, base_high, coef, weight):
    nx = lax.axis_size("gx")
    ix = lax.axis_index("gx")
    X = stage.shape[1]
    up = [(i, i + 1) for i in range(nx - 1)]
    down = [(i + 1, i) for i in range(nx - 1)]
    tall = y_extended(stage)
    zero_plane = jnp.zeros_like(stage[:, :1])
    part_top = operator(tall[:, X - 1:], stage[:, X - 2:X - 1], zero_plane, cut(coef, X - 1, X))
    part_bottom = operator(tall[:, :1], zero_plane, stage[:, 1:2], cut(coef, 0, 1))
    from_low = lax.ppermute(jnp.concatenate([stage[:, X - 1:], part_top]), "gx", up)
    from_high = lax.ppermute(jnp.concatenate([stage[:, :1], part_bottom]), "gx", down)
    stage_low, part_low = from_low[:2], from_low[2:]
    stage_high, part_high = from_high[:2], from_high[2:]
    if base_low is None:
        base_low, base_high = stage_low, stage_high
    section = operator(tall, stage_low, stage_high, coef)
    section_low = part_low + across(stage[:, :1])
    section_high = part_high + across(stage[:, X - 1:])
    nxt = base + weight * section
    nxt_low = jnp.where(ix > 0, base_low + weight * section_low, 0.0)
    nxt_high = jnp.where(ix < nx - 1, base_high + weight * section_high, 0.0)
    section_next = operator(y_extended(nxt), nxt_low, nxt_high, coef)
    return section, section_next, base_low, base_high


def rk_step(field, coef):
    section_one, section_two, low, high = stage_pair(
        field, field, None, None, coef, 0.5 * STEP_SIZE
    )
    stage_three = field + 0.5 * STEP_SIZE * section_two
    section_three, section_four, _, _ = stage_pair(
        stage_three, field, low, high, coef, STEP_SIZE
    )
    return field + STEP_SIZE / 6.0 * (
        section_one + 2.0 * section_two + 2.0 * section_three + section_four
    )


def row_terms(field, psi, profile):
    intersection = field[0] * psi[1] - field[1] * psi[0]
    summed = jnp.sum(intersection * profile[:, None, None], axis=0)
    return summed.reshape(summed.shape[0] // 2, 2, summed.shape[1]).sum(axis=1)


def on_device(chi_final, psi_late, psi_early, trap, controls):
    planes = chi_final.shape[1]
    width_y = chi_final.shape[2]
    depth = chi_final.shape[3]
    total_x = planes * lax.axis_size("gx")
    total_y = width_y * lax.axis_size("gy")
    first = lax.axis_index("gx") * planes
    x_index = (first + jnp.arange(planes, dtype=jnp.int32)).astype(jnp.float32)
    profile = 1.0 + 0.5 * jnp.cos(2.0 * math.pi * x_index / float(total_x))
    coef_late = coefficients(psi_late, trap, controls[1], profile)
    coef_early = coefficients(psi_early, trap, controls[0], profile)
    chi_late = rk_step(chi_final, coef_late)
    chi_start = rk_step(chi_late, coef_early)
    rows_late = row_terms(chi_late, psi_late, profile)
    rows_early = row_terms(chi_start, psi_early, profile)
    local_sq = jnp.sum(chi_start * chi_start)
    extra = jnp.zeros((1, rows_early.shape[1]), jnp.float32).at[0, 0].set(local_sq)
    packed = axis_sum(jnp.concatenate([rows_early, rows_late, extra], axis=0), "gx")
    squares = axis_sum(packed[-1, 0], "gy")
    half = rows_early.shape[0]
    rows_sum = jnp.stack([packed[:half], packed[half:2 * half]])
    power = squares / float(total_x * total_y * depth)
    grad_rows = rows_sum / jnp.sqrt(float(total_x) * (power + 1e-06))
    return (chi_start, grad_rows, jnp.reshape(power, (1,)))


def solution(mesh):
    placed = (
        P(None, ("starts", "gx"), "gy", None),
        P(None, ("starts", "gx"), "gy", None),
        P(None, ("starts", "gx"), "gy", None),
        P("gx", "gy", None),
        P("starts", "gy", None),
    )
    return jax.shard_map(
        on_device,
        mesh=mesh,
        in_specs=placed,
        out_specs=(P(None, ("starts", "gx"), "gy", None), P("starts", "gy", None), P("starts")),
        check_vma=False,
    )
```

```python
import math

import jax
import jax.numpy as jnp
from jax import lax
from jax.sharding import PartitionSpec as P

COUPLING = 1.0
STEP_SIZE = 0.2


def axis_sum(value, axis):
    count = lax.axis_size(axis)
    if count & (count - 1):
        return lax.psum(value, axis)
    step = 1
    while step < count:
        pairs = [(i, i ^ step) for i in range(count)]
        value = value + lax.ppermute(value, axis, pairs)
        step *= 2
    return value


def gx_total(value):
    count = lax.axis_size("gx")
    if count > 8 or count % 2:
        return axis_sum(value, "gx")
    pair = value + lax.ppermute(value, "gx", [(i, i ^ 1) for i in range(count)])
    groups = count // 2
    if groups == 1:
        return pair
    fetched = [pair] + [
        lax.ppermute(pair, "gx", [(i, i ^ (2 * k)) for i in range(count)])
        for k in range(1, groups)
    ]
    stacked = jnp.stack(fetched)
    mine = lax.axis_index("gx") // 2
    total = lax.dynamic_index_in_dim(stacked, mine, keepdims=False)
    for j in range(1, groups):
        total = total + lax.dynamic_index_in_dim(stacked, mine ^ j, keepdims=False)
    return total


def y_extended(block):
    ny = lax.axis_size("gy")
    iy = lax.axis_index("gy")
    Y = block.shape[2]
    if ny == 2:
        strip = lax.dynamic_slice_in_dim(block, (1 - iy) * (Y - 1), 1, axis=2)
        other = lax.ppermute(strip, "gy", [(0, 1), (1, 0)])
        zero = jnp.zeros_like(other)
        below = jnp.where(iy == 1, other, zero)
        above = jnp.where(iy == 0, other, zero)
    else:
        below = lax.ppermute(block[:, :, Y - 1:], "gy", [(j, j + 1) for j in range(ny - 1)])
        above = lax.ppermute(block[:, :, :1], "gy", [(j + 1, j) for j in range(ny - 1)])
    return jnp.concatenate([below, block, above], axis=2)


def coefficients(psi, trap, control, profile):
    real_part = psi[0]
    imag_part = psi[1]
    fine_control = jnp.repeat(control, 2, axis=0)
    potential = trap + profile[:, None, None] * fine_control[None, :, :]
    weight = potential + 2.0 * COUPLING * (real_part * real_part + imag_part * imag_part)
    mix_a = COUPLING * (real_part * real_part - imag_part * imag_part)
    mix_b = 2.0 * COUPLING * real_part * imag_part
    return (weight, mix_a, mix_b)


def apply_coef(lapl, field, coef):
    weight, mix_a, mix_b = coef
    real_part = field[0]
    imag_part = field[1]
    upper = -0.5 * lapl[0] + (weight + mix_a) * real_part + mix_b * imag_part
    lower = -0.5 * lapl[1] + mix_b * real_part + (weight - mix_a) * imag_part
    return jnp.stack([-lower, upper])


def operator(tall, x_low, x_high, coef):
    field = tall[:, :, 1:-1]
    x_padded = jnp.concatenate([x_low, field, x_high], axis=1)
    z_padded = jnp.pad(field, ((0, 0), (0, 0), (0, 0), (1, 1)))
    total = x_padded[:, 2:] + x_padded[:, :-2]
    total = total + tall[:, :, 2:] + tall[:, :, :-2]
    total = total + z_padded[:, :, :, 2:] + z_padded[:, :, :, :-2]
    lapl = total - 6.0 * field
    return apply_coef(lapl, field, coef)


def cut(coef, lo, hi):
    return tuple(c[lo:hi] for c in coef)


def across(plane):
    return jnp.stack([0.5 * plane[1], -0.5 * plane[0]])


def stage_pair(stage, base, base_low, base_high, coef, weight):
    nx = lax.axis_size("gx")
    ix = lax.axis_index("gx")
    X = stage.shape[1]
    up = [(i, i + 1) for i in range(nx - 1)]
    down = [(i + 1, i) for i in range(nx - 1)]
    tall = y_extended(stage)
    zero_plane = jnp.zeros_like(stage[:, :1])
    part_top = operator(tall[:, X - 1:], stage[:, X - 2:X - 1], zero_plane, cut(coef, X - 1, X))
    part_bottom = operator(tall[:, :1], zero_plane, stage[:, 1:2], cut(coef, 0, 1))
    from_low = lax.ppermute(jnp.concatenate([stage[:, X - 1:], part_top]), "gx", up)
    from_high = lax.ppermute(jnp.concatenate([stage[:, :1], part_bottom]), "gx", down)
    stage_low, part_low = from_low[:2], from_low[2:]
    stage_high, part_high = from_high[:2], from_high[2:]
    if base_low is None:
        base_low, base_high = stage_low, stage_high
    section = operator(tall, stage_low, stage_high, coef)
    section_low = part_low + across(stage[:, :1])
    section_high = part_high + across(stage[:, X - 1:])
    nxt = base + weight * section
    nxt_low = jnp.where(ix > 0, base_low + weight * section_low, 0.0)
    nxt_high = jnp.where(ix < nx - 1, base_high + weight * section_high, 0.0)
    section_next = operator(y_extended(nxt), nxt_low, nxt_high, coef)
    return section, section_next, base_low, base_high


def rk_step(field, coef):
    section_one, section_two, low, high = stage_pair(
        field, field, None, None, coef, 0.5 * STEP_SIZE
    )
    stage_three = field + 0.5 * STEP_SIZE * section_two
    section_three, section_four, _, _ = stage_pair(
        stage_three, field, low, high, coef, STEP_SIZE
    )
    return field + STEP_SIZE / 6.0 * (
        section_one + 2.0 * section_two + 2.0 * section_three + section_four
    )


def row_terms(field, psi, profile):
    intersection = field[0] * psi[1] - field[1] * psi[0]
    summed = jnp.sum(intersection * profile[:, None, None], axis=0)
    return summed.reshape(summed.shape[0] // 2, 2, summed.shape[1]).sum(axis=1)


def on_device(chi_final, psi_late, psi_early, trap, controls):
    planes = chi_final.shape[1]
    width_y = chi_final.shape[2]
    depth = chi_final.shape[3]
    total_x = planes * lax.axis_size("gx")
    total_y = width_y * lax.axis_size("gy")
    first = lax.axis_index("gx") * planes
    x_index = (first + jnp.arange(planes, dtype=jnp.int32)).astype(jnp.float32)
    profile = 1.0 + 0.5 * jnp.cos(2.0 * math.pi * x_index / float(total_x))
    coef_late = coefficients(psi_late, trap, controls[1], profile)
    coef_early = coefficients(psi_early, trap, controls[0], profile)
    chi_late = rk_step(chi_final, coef_late)
    chi_start = rk_step(chi_late, coef_early)
    rows_late = row_terms(chi_late, psi_late, profile)
    rows_early = row_terms(chi_start, psi_early, profile)
    local_sq = axis_sum(jnp.sum(chi_start * chi_start), "gy")
    extra = jnp.zeros((1, rows_early.shape[1]), jnp.float32).at[0, 0].set(local_sq)
    packed = gx_total(jnp.concatenate([rows_early, rows_late, extra], axis=0))
    squares = packed[-1, 0]
    half = rows_early.shape[0]
    rows_sum = jnp.stack([packed[:half], packed[half:2 * half]])
    power = squares / float(total_x * total_y * depth)
    grad_rows = rows_sum / jnp.sqrt(float(total_x) * (power + 1e-06))
    return (chi_start, grad_rows, jnp.reshape(power, (1,)))


def solution(mesh):
    placed = (
        P(None, ("starts", "gx"), "gy", None),
        P(None, ("starts", "gx"), "gy", None),
        P(None, ("starts", "gx"), "gy", None),
        P("gx", "gy", None),
        P("starts", "gy", None),
    )
    return jax.shard_map(
        on_device,
        mesh=mesh,
        in_specs=placed,
        out_specs=(P(None, ("starts", "gx"), "gy", None), P("starts", "gy", None), P("starts")),
        check_vma=False,
    )
```

```python
import math

import jax
import jax.numpy as jnp
from jax import lax
from jax.sharding import PartitionSpec as P

COUPLING = 1.0
STEP_SIZE = 0.2


def axis_sum(value, axis):
    count = lax.axis_size(axis)
    if count & (count - 1):
        return lax.psum(value, axis)
    step = 1
    while step < count:
        pairs = [(i, i ^ step) for i in range(count)]
        value = value + lax.ppermute(value, axis, pairs)
        step *= 2
    return value


def gx_total(value):
    count = lax.axis_size("gx")
    if count > 8 or count % 2:
        return axis_sum(value, "gx")
    pair = value + lax.ppermute(value, "gx", [(i, i ^ 1) for i in range(count)])
    groups = count // 2
    if groups == 1:
        return pair
    fetched = [pair] + [
        lax.ppermute(pair, "gx", [(i, i ^ (2 * k)) for i in range(count)])
        for k in range(1, groups)
    ]
    stacked = jnp.stack(fetched)
    mine = lax.axis_index("gx") // 2
    total = lax.dynamic_index_in_dim(stacked, mine, keepdims=False)
    for j in range(1, groups):
        total = total + lax.dynamic_index_in_dim(stacked, mine ^ j, keepdims=False)
    return total


def y_extended(block):
    ny = lax.axis_size("gy")
    iy = lax.axis_index("gy")
    Y = block.shape[2]
    if ny == 2:
        strip = lax.dynamic_slice_in_dim(block, (1 - iy) * (Y - 1), 1, axis=2)
        other = lax.ppermute(strip, "gy", [(0, 1), (1, 0)])
        zero = jnp.zeros_like(other)
        below = jnp.where(iy == 1, other, zero)
        above = jnp.where(iy == 0, other, zero)
    else:
        below = lax.ppermute(block[:, :, Y - 1:], "gy", [(j, j + 1) for j in range(ny - 1)])
        above = lax.ppermute(block[:, :, :1], "gy", [(j + 1, j) for j in range(ny - 1)])
    return jnp.concatenate([below, block, above], axis=2)


def coefficients(psi, trap, control, profile):
    real_part = psi[0]
    imag_part = psi[1]
    fine_control = jnp.repeat(control, 2, axis=0)
    potential = trap + profile[:, None, None] * fine_control[None, :, :]
    weight = potential + 2.0 * COUPLING * (real_part * real_part + imag_part * imag_part)
    mix_a = COUPLING * (real_part * real_part - imag_part * imag_part)
    mix_b = 2.0 * COUPLING * real_part * imag_part
    return (weight, mix_a, mix_b)


def apply_coef(lapl, field, coef):
    weight, mix_a, mix_b = coef
    real_part = field[0]
    imag_part = field[1]
    upper = -0.5 * lapl[0] + (weight + mix_a) * real_part + mix_b * imag_part
    lower = -0.5 * lapl[1] + mix_b * real_part + (weight - mix_a) * imag_part
    return jnp.stack([-lower, upper])


def operator(tall, x_low, x_high, coef):
    field = tall[:, :, 1:-1]
    x_padded = jnp.concatenate([x_low, field, x_high], axis=1)
    z_padded = jnp.pad(field, ((0, 0), (0, 0), (0, 0), (1, 1)))
    total = x_padded[:, 2:] + x_padded[:, :-2]
    total = total + tall[:, :, 2:] + tall[:, :, :-2]
    total = total + z_padded[:, :, :, 2:] + z_padded[:, :, :, :-2]
    lapl = total - 6.0 * field
    return apply_coef(lapl, field, coef)


def across(plane):
    return jnp.stack([0.5 * plane[1], -0.5 * plane[0]])


def stage_pair(stage, base, base_low, base_high, coef, weight):
    nx = lax.axis_size("gx")
    ix = lax.axis_index("gx")
    X = stage.shape[1]
    up = [(i, i + 1) for i in range(nx - 1)]
    down = [(i + 1, i) for i in range(nx - 1)]
    tall = y_extended(stage)
    zero_plane = jnp.zeros_like(stage[:, :1])
    part_top = operator(tall[:, X - 1:], stage[:, X - 2:X - 1], zero_plane, coef["top"])
    part_bottom = operator(tall[:, :1], zero_plane, stage[:, 1:2], coef["bottom"])
    from_low = lax.ppermute(jnp.concatenate([stage[:, X - 1:], part_top]), "gx", up)
    from_high = lax.ppermute(jnp.concatenate([stage[:, :1], part_bottom]), "gx", down)
    stage_low, part_low = from_low[:2], from_low[2:]
    stage_high, part_high = from_high[:2], from_high[2:]
    if base_low is None:
        base_low, base_high = stage_low, stage_high
    section = operator(tall, stage_low, stage_high, coef["all"])
    section_low = part_low + across(stage[:, :1])
    section_high = part_high + across(stage[:, X - 1:])
    nxt = base + weight * section
    nxt_low = jnp.where(ix > 0, base_low + weight * section_low, 0.0)
    nxt_high = jnp.where(ix < nx - 1, base_high + weight * section_high, 0.0)
    section_next = operator(y_extended(nxt), nxt_low, nxt_high, coef["all"])
    return section, section_next, base_low, base_high


def rk_step(field, coef):
    section_one, section_two, low, high = stage_pair(
        field, field, None, None, coef, 0.5 * STEP_SIZE
    )
    stage_three = field + 0.5 * STEP_SIZE * section_two
    section_three, section_four, _, _ = stage_pair(
        stage_three, field, low, high, coef, STEP_SIZE
    )
    return field + STEP_SIZE / 6.0 * (
        section_one + 2.0 * section_two + 2.0 * section_three + section_four
    )


def row_terms(field, psi, profile):
    intersection = field[0] * psi[1] - field[1] * psi[0]
    summed = jnp.sum(intersection * profile[:, None, None], axis=0)
    return summed.reshape(summed.shape[0] // 2, 2, summed.shape[1]).sum(axis=1)


def on_device(chi_final, psi_late, psi_early, trap, controls):
    planes = chi_final.shape[1]
    width_y = chi_final.shape[2]
    depth = chi_final.shape[3]
    total_x = planes * lax.axis_size("gx")
    total_y = width_y * lax.axis_size("gy")
    first = lax.axis_index("gx") * planes
    x_index = (first + jnp.arange(planes, dtype=jnp.int32)).astype(jnp.float32)
    profile = 1.0 + 0.5 * jnp.cos(2.0 * math.pi * x_index / float(total_x))
    def coefficient_set(psi, control):
        return {
            "all": coefficients(psi, trap, control, profile),
            "top": coefficients(psi[:, planes - 1:], trap[planes - 1:], control, profile[planes - 1:]),
            "bottom": coefficients(psi[:, :1], trap[:1], control, profile[:1]),
        }

    coef_late = coefficient_set(psi_late, controls[1])
    coef_early = coefficient_set(psi_early, controls[0])
    chi_late = rk_step(chi_final, coef_late)
    chi_start = rk_step(chi_late, coef_early)
    local_sq = axis_sum(jnp.sum(chi_start * chi_start), "gy")
    rows_late = row_terms(chi_late, psi_late, profile)
    rows_early = row_terms(chi_start, psi_early, profile)
    extra = jnp.zeros((1, rows_early.shape[1]), jnp.float32).at[0, 0].set(local_sq)
    packed = gx_total(jnp.concatenate([rows_early, rows_late, extra], axis=0))
    squares = packed[-1, 0]
    half = rows_early.shape[0]
    rows_sum = jnp.stack([packed[:half], packed[half:2 * half]])
    power = squares / float(total_x * total_y * depth)
    grad_rows = rows_sum / jnp.sqrt(float(total_x) * (power + 1e-06))
    return (chi_start, grad_rows, jnp.reshape(power, (1,)))


def solution(mesh):
    placed = (
        P(None, ("starts", "gx"), "gy", None),
        P(None, ("starts", "gx"), "gy", None),
        P(None, ("starts", "gx"), "gy", None),
        P("gx", "gy", None),
        P("starts", "gy", None),
    )
    return jax.shard_map(
        on_device,
        mesh=mesh,
        in_specs=placed,
        out_specs=(P(None, ("starts", "gx"), "gy", None), P("starts", "gy", None), P("starts")),
        check_vma=False,
    )
```

```python
import math

import jax
import jax.numpy as jnp
from jax import lax
from jax.sharding import PartitionSpec as P

COUPLING = 1.0
STEP_SIZE = 0.2


def axis_sum(value, axis):
    count = lax.axis_size(axis)
    if count & (count - 1):
        return lax.psum(value, axis)
    step = 1
    while step < count:
        pairs = [(i, i ^ step) for i in range(count)]
        value = value + lax.ppermute(value, axis, pairs)
        step *= 2
    return value


def gx_total(value):
    count = lax.axis_size("gx")
    if count > 8 or count % 2:
        return axis_sum(value, "gx")
    pair = value + lax.ppermute(value, "gx", [(i, i ^ 1) for i in range(count)])
    groups = count // 2
    if groups == 1:
        return pair
    fetched = [pair] + [
        lax.ppermute(pair, "gx", [(i, i ^ (2 * k)) for i in range(count)])
        for k in range(1, groups)
    ]
    stacked = jnp.stack(fetched)
    mine = lax.axis_index("gx") // 2
    total = lax.dynamic_index_in_dim(stacked, mine, keepdims=False)
    for j in range(1, groups):
        total = total + lax.dynamic_index_in_dim(stacked, mine ^ j, keepdims=False)
    return total


def y_extended(block):
    ny = lax.axis_size("gy")
    iy = lax.axis_index("gy")
    Y = block.shape[2]
    if ny == 2:
        strip = lax.dynamic_slice_in_dim(block, (1 - iy) * (Y - 1), 1, axis=2)
        other = lax.ppermute(strip, "gy", [(0, 1), (1, 0)])
        zero = jnp.zeros_like(other)
        below = jnp.where(iy == 1, other, zero)
        above = jnp.where(iy == 0, other, zero)
    else:
        below = lax.ppermute(block[:, :, Y - 1:], "gy", [(j, j + 1) for j in range(ny - 1)])
        above = lax.ppermute(block[:, :, :1], "gy", [(j + 1, j) for j in range(ny - 1)])
    return jnp.concatenate([below, block, above], axis=2)


def coefficients(psi, trap, control, profile):
    real_part = psi[0]
    imag_part = psi[1]
    fine_control = jnp.repeat(control, 2, axis=0)
    potential = trap + profile[:, None, None] * fine_control[None, :, :]
    weight = potential + 2.0 * COUPLING * (real_part * real_part + imag_part * imag_part)
    mix_a = COUPLING * (real_part * real_part - imag_part * imag_part)
    mix_b = 2.0 * COUPLING * real_part * imag_part
    return (weight, mix_a, mix_b)


def apply_coef(lapl, field, coef):
    weight, mix_a, mix_b = coef
    real_part = field[0]
    imag_part = field[1]
    upper = -0.5 * lapl[0] + (weight + mix_a) * real_part + mix_b * imag_part
    lower = -0.5 * lapl[1] + mix_b * real_part + (weight - mix_a) * imag_part
    return jnp.stack([-lower, upper])


def operator(tall, x_low, x_high, coef):
    field = tall[:, :, 1:-1]
    x_padded = jnp.concatenate([x_low, field, x_high], axis=1)
    z_padded = jnp.pad(field, ((0, 0), (0, 0), (0, 0), (1, 1)))
    total = x_padded[:, 2:] + x_padded[:, :-2]
    total = total + tall[:, :, 2:] + tall[:, :, :-2]
    total = total + z_padded[:, :, :, 2:] + z_padded[:, :, :, :-2]
    lapl = total - 6.0 * field
    return apply_coef(lapl, field, coef)


def cut(coef, lo, hi):
    return tuple(c[lo:hi] for c in coef)


def across(plane):
    return jnp.stack([0.5 * plane[1], -0.5 * plane[0]])


def zero_extended(block):
    zero = jnp.zeros_like(block[:, :, :1])
    return jnp.concatenate([zero, block, zero], axis=2)


def stage_pair(stage, base, base_low, base_high, coef, weight, extend_y):
    nx = lax.axis_size("gx")
    ix = lax.axis_index("gx")
    X = stage.shape[1]
    up = [(i, i + 1) for i in range(nx - 1)]
    down = [(i + 1, i) for i in range(nx - 1)]
    tall = extend_y(stage)
    zero_plane = jnp.zeros_like(stage[:, :1])
    part_top = operator(tall[:, X - 1:], stage[:, X - 2:X - 1], zero_plane, cut(coef, X - 1, X))
    part_bottom = operator(tall[:, :1], zero_plane, stage[:, 1:2], cut(coef, 0, 1))
    from_low = lax.ppermute(jnp.concatenate([stage[:, X - 1:], part_top]), "gx", up)
    from_high = lax.ppermute(jnp.concatenate([stage[:, :1], part_bottom]), "gx", down)
    stage_low, part_low = from_low[:2], from_low[2:]
    stage_high, part_high = from_high[:2], from_high[2:]
    if base_low is None:
        base_low, base_high = stage_low, stage_high
    section = operator(tall, stage_low, stage_high, coef)
    section_low = part_low + across(stage[:, :1])
    section_high = part_high + across(stage[:, X - 1:])
    nxt = base + weight * section
    nxt_low = jnp.where(ix > 0, base_low + weight * section_low, 0.0)
    nxt_high = jnp.where(ix < nx - 1, base_high + weight * section_high, 0.0)
    section_next = operator(extend_y(nxt), nxt_low, nxt_high, coef)
    return section, section_next, base_low, base_high


CHAIN = 40


def rk_chain(field, coef, extend_y):
    section_one, section_two, low, high = stage_pair(
        field, field, None, None, coef, 0.5 * STEP_SIZE, extend_y
    )
    stage_three = field + 0.5 * STEP_SIZE * section_two
    section_three, section_four, _, _ = stage_pair(
        stage_three, field, low, high, coef, STEP_SIZE, extend_y
    )
    return field + STEP_SIZE / 6.0 * (
        section_one + 2.0 * section_two + 2.0 * section_three + section_four
    )


def rk_step(field, coef):
    rows = field.shape[2]
    half = rows // 2
    if lax.axis_size("gy") != 2 or rows % 2 or CHAIN > rows or CHAIN - half < 4:
        return rk_chain(field, coef, y_extended)
    iy = lax.axis_index("gy")
    spare = CHAIN - half
    chains = []
    for start, keep, extend_y in (
        ((1 - iy) * (rows - CHAIN), (1 - iy) * spare, y_extended),
        (iy * (rows - CHAIN), iy * spare, zero_extended),
    ):
        part = lax.dynamic_slice_in_dim(field, start, CHAIN, axis=2)
        part_coef = tuple(lax.dynamic_slice_in_dim(c, start, CHAIN, axis=1) for c in coef)
        chains.append((part, part_coef, extend_y, keep))
    (fa, ca, ea, ka), (fb, cb, eb, kb) = chains
    a1, a2, a_low, a_high = stage_pair(fa, fa, None, None, ca, 0.5 * STEP_SIZE, ea)
    fb, a1 = lax.optimization_barrier((fb, a1))
    b1, b2, b_low, b_high = stage_pair(fb, fb, None, None, cb, 0.5 * STEP_SIZE, eb)
    a3, a4, _, _ = stage_pair(fa + 0.5 * STEP_SIZE * a2, fa, a_low, a_high, ca, STEP_SIZE, ea)
    b_three, a3 = lax.optimization_barrier((fb + 0.5 * STEP_SIZE * b2, a3))
    b3, b4, _, _ = stage_pair(b_three, fb, b_low, b_high, cb, STEP_SIZE, eb)
    kept = []
    for f, s1, s2, s3, s4, keep in ((fa, a1, a2, a3, a4, ka), (fb, b1, b2, b3, b4, kb)):
        out = f + STEP_SIZE / 6.0 * (s1 + 2.0 * s2 + 2.0 * s3 + s4)
        kept.append(lax.dynamic_slice_in_dim(out, keep, half, axis=2))
    near, far = kept
    return jnp.where(
        iy == 0,
        jnp.concatenate([far, near], axis=2),
        jnp.concatenate([near, far], axis=2),
    )


def row_terms(field, psi, profile):
    intersection = field[0] * psi[1] - field[1] * psi[0]
    summed = jnp.sum(intersection * profile[:, None, None], axis=0)
    return summed.reshape(summed.shape[0] // 2, 2, summed.shape[1]).sum(axis=1)


def on_device(chi_final, psi_late, psi_early, trap, controls):
    planes = chi_final.shape[1]
    width_y = chi_final.shape[2]
    depth = chi_final.shape[3]
    total_x = planes * lax.axis_size("gx")
    total_y = width_y * lax.axis_size("gy")
    first = lax.axis_index("gx") * planes
    x_index = (first + jnp.arange(planes, dtype=jnp.int32)).astype(jnp.float32)
    profile = 1.0 + 0.5 * jnp.cos(2.0 * math.pi * x_index / float(total_x))
    coef_late = coefficients(psi_late, trap, controls[1], profile)
    coef_early = coefficients(psi_early, trap, controls[0], profile)
    chi_late = rk_step(chi_final, coef_late)
    chi_start = rk_step(chi_late, coef_early)
    rows_late = row_terms(chi_late, psi_late, profile)
    rows_early = row_terms(chi_start, psi_early, profile)
    local_sq = axis_sum(jnp.sum(chi_start * chi_start), "gy")
    extra = jnp.zeros((1, rows_early.shape[1]), jnp.float32).at[0, 0].set(local_sq)
    packed = gx_total(jnp.concatenate([rows_early, rows_late, extra], axis=0))
    squares = packed[-1, 0]
    half = rows_early.shape[0]
    rows_sum = jnp.stack([packed[:half], packed[half:2 * half]])
    power = squares / float(total_x * total_y * depth)
    grad_rows = rows_sum / jnp.sqrt(float(total_x) * (power + 1e-06))
    return (chi_start, grad_rows, jnp.reshape(power, (1,)))


def solution(mesh):
    placed = (
        P(None, ("starts", "gx"), "gy", None),
        P(None, ("starts", "gx"), "gy", None),
        P(None, ("starts", "gx"), "gy", None),
        P("gx", "gy", None),
        P("starts", "gy", None),
    )
    return jax.shard_map(
        on_device,
        mesh=mesh,
        in_specs=placed,
        out_specs=(P(None, ("starts", "gx"), "gy", None), P("starts", "gy", None), P("starts")),
        check_vma=False,
    )
```

```python
import math

import jax
import jax.numpy as jnp
from jax import lax
from jax.sharding import PartitionSpec as P

COUPLING = 1.0
STEP_SIZE = 0.2


def axis_sum(value, axis):
    count = lax.axis_size(axis)
    if count & (count - 1):
        return lax.psum(value, axis)
    step = 1
    while step < count:
        pairs = [(i, i ^ step) for i in range(count)]
        value = value + lax.ppermute(value, axis, pairs)
        step *= 2
    return value


def gx_total(value):
    count = lax.axis_size("gx")
    if count > 8 or count % 2:
        return axis_sum(value, "gx")
    pair = value + lax.ppermute(value, "gx", [(i, i ^ 1) for i in range(count)])
    groups = count // 2
    if groups == 1:
        return pair
    fetched = [pair] + [
        lax.ppermute(pair, "gx", [(i, i ^ (2 * k)) for i in range(count)])
        for k in range(1, groups)
    ]
    stacked = jnp.stack(fetched)
    mine = lax.axis_index("gx") // 2
    total = lax.dynamic_index_in_dim(stacked, mine, keepdims=False)
    for j in range(1, groups):
        total = total + lax.dynamic_index_in_dim(stacked, mine ^ j, keepdims=False)
    return total


def y_extended(block):
    ny = lax.axis_size("gy")
    iy = lax.axis_index("gy")
    Y = block.shape[2]
    if ny == 2:
        strip = lax.dynamic_slice_in_dim(block, (1 - iy) * (Y - 1), 1, axis=2)
        other = lax.ppermute(strip, "gy", [(0, 1), (1, 0)])
        zero = jnp.zeros_like(other)
        below = jnp.where(iy == 1, other, zero)
        above = jnp.where(iy == 0, other, zero)
    else:
        below = lax.ppermute(block[:, :, Y - 1:], "gy", [(j, j + 1) for j in range(ny - 1)])
        above = lax.ppermute(block[:, :, :1], "gy", [(j + 1, j) for j in range(ny - 1)])
    return jnp.concatenate([below, block, above], axis=2)


def coefficients(psi, trap, control, profile):
    real_part = psi[0]
    imag_part = psi[1]
    fine_control = jnp.repeat(control, 2, axis=0)
    potential = trap + profile[:, None, None] * fine_control[None, :, :]
    weight = potential + 2.0 * COUPLING * (real_part * real_part + imag_part * imag_part)
    mix_a = COUPLING * (real_part * real_part - imag_part * imag_part)
    mix_b = 2.0 * COUPLING * real_part * imag_part
    return (weight, mix_a, mix_b)


def apply_coef(lapl, field, coef):
    weight, mix_a, mix_b = coef
    real_part = field[0]
    imag_part = field[1]
    upper = -0.5 * lapl[0] + (weight + mix_a) * real_part + mix_b * imag_part
    lower = -0.5 * lapl[1] + mix_b * real_part + (weight - mix_a) * imag_part
    return jnp.stack([-lower, upper])


def operator(tall, x_low, x_high, coef):
    field = tall[:, :, 1:-1]
    x_padded = jnp.concatenate([x_low, field, x_high], axis=1)
    z_padded = jnp.pad(field, ((0, 0), (0, 0), (0, 0), (1, 1)))
    total = x_padded[:, 2:] + x_padded[:, :-2]
    total = total + tall[:, :, 2:] + tall[:, :, :-2]
    total = total + z_padded[:, :, :, 2:] + z_padded[:, :, :, :-2]
    lapl = total - 6.0 * field
    return apply_coef(lapl, field, coef)


def cut(coef, lo, hi):
    return tuple(c[lo:hi] for c in coef)


def across(plane):
    return jnp.stack([0.5 * plane[1], -0.5 * plane[0]])


def with_partner_row(block, row):
    iy = lax.axis_index("gy")
    zero = jnp.zeros_like(row)
    below = jnp.where(iy == 1, row, zero)
    above = jnp.where(iy == 0, row, zero)
    return jnp.concatenate([below, block, above], axis=2)


def edge_rows(block, offset=0):
    iy = lax.axis_index("gy")
    Y = block.shape[2]
    start = (1 - iy) * (Y - 1 - offset) + iy * offset
    return lax.dynamic_slice_in_dim(block, start, 1, axis=2)


def partner_coef(coef):
    rows = jnp.stack([edge_rows(c[:, None])[:, 0] for c in coef])
    got = lax.ppermute(rows, "gy", [(0, 1), (1, 0)])
    return tuple(got[k] for k in range(len(coef)))


def stage_pair(stage, base, base_low, base_high, coef, weight, tall=None, ahead=None):
    nx = lax.axis_size("gx")
    ix = lax.axis_index("gx")
    iy = lax.axis_index("gy")
    X = stage.shape[1]
    up = [(i, i + 1) for i in range(nx - 1)]
    down = [(i + 1, i) for i in range(nx - 1)]
    if tall is None:
        tall = y_extended(stage)
    zero_plane = jnp.zeros_like(stage[:, :1])
    part_top = operator(tall[:, X - 1:], stage[:, X - 2:X - 1], zero_plane, cut(coef, X - 1, X))
    part_bottom = operator(tall[:, :1], zero_plane, stage[:, 1:2], cut(coef, 0, 1))
    from_low = lax.ppermute(jnp.concatenate([stage[:, X - 1:], part_top]), "gx", up)
    from_high = lax.ppermute(jnp.concatenate([stage[:, :1], part_bottom]), "gx", down)
    stage_low, part_low = from_low[:2], from_low[2:]
    stage_high, part_high = from_high[:2], from_high[2:]
    if base_low is None:
        base_low, base_high = stage_low, stage_high
    section = operator(tall, stage_low, stage_high, coef)
    section_low = part_low + across(stage[:, :1])
    section_high = part_high + across(stage[:, X - 1:])
    nxt = base + weight * section
    nxt_low = jnp.where(ix > 0, base_low + weight * section_low, 0.0)
    nxt_high = jnp.where(ix < nx - 1, base_high + weight * section_high, 0.0)
    if ahead is None:
        section_next = operator(y_extended(nxt), nxt_low, nxt_high, coef)
        return section, section_next, base_low, base_high, None
    next_weight, coef_partner = ahead
    mine = edge_rows(nxt)
    pack = jnp.concatenate(
        [mine, edge_rows(nxt, 1), edge_rows(nxt_low), edge_rows(nxt_high)], axis=1
    )
    got = lax.ppermute(pack, "gy", [(0, 1), (1, 0)])
    their, their_inner = got[:, :X], got[:, X:2 * X]
    their_low, their_high = got[:, 2 * X:2 * X + 1], got[:, 2 * X + 1:2 * X + 2]
    section_next = operator(with_partner_row(nxt, their), nxt_low, nxt_high, coef)
    slab = jnp.where(
        iy == 0,
        jnp.concatenate([mine, their, their_inner], axis=2),
        jnp.concatenate([their_inner, their, mine], axis=2),
    )
    their_section = operator(slab, their_low, their_high, coef_partner)
    their_base = jnp.where(iy == 1, tall[:, :, :1], tall[:, :, -1:])
    their_next = their_base + next_weight * their_section
    return section, section_next, base_low, base_high, their_next


def rk_step(field, coef):
    fast = lax.axis_size("gy") == 2 and field.shape[2] >= 3
    ahead = (0.5 * STEP_SIZE, partner_coef(coef)) if fast else None
    section_one, section_two, low, high, their_three = stage_pair(
        field, field, None, None, coef, 0.5 * STEP_SIZE, ahead=ahead
    )
    stage_three = field + 0.5 * STEP_SIZE * section_two
    tall_three = with_partner_row(stage_three, their_three) if fast else None
    section_three, section_four, _, _, _ = stage_pair(
        stage_three, field, low, high, coef, STEP_SIZE, tall=tall_three
    )
    return field + STEP_SIZE / 6.0 * (
        section_one + 2.0 * section_two + 2.0 * section_three + section_four
    )


def row_terms(field, psi, profile):
    intersection = field[0] * psi[1] - field[1] * psi[0]
    summed = jnp.sum(intersection * profile[:, None, None], axis=0)
    return summed.reshape(summed.shape[0] // 2, 2, summed.shape[1]).sum(axis=1)


def on_device(chi_final, psi_late, psi_early, trap, controls):
    planes = chi_final.shape[1]
    width_y = chi_final.shape[2]
    depth = chi_final.shape[3]
    total_x = planes * lax.axis_size("gx")
    total_y = width_y * lax.axis_size("gy")
    first = lax.axis_index("gx") * planes
    x_index = (first + jnp.arange(planes, dtype=jnp.int32)).astype(jnp.float32)
    profile = 1.0 + 0.5 * jnp.cos(2.0 * math.pi * x_index / float(total_x))
    coef_late = coefficients(psi_late, trap, controls[1], profile)
    coef_early = coefficients(psi_early, trap, controls[0], profile)
    chi_late = rk_step(chi_final, coef_late)
    chi_start = rk_step(chi_late, coef_early)
    rows_late = row_terms(chi_late, psi_late, profile)
    rows_early = row_terms(chi_start, psi_early, profile)
    local_sq = axis_sum(jnp.sum(chi_start * chi_start), "gy")
    extra = jnp.zeros((1, rows_early.shape[1]), jnp.float32).at[0, 0].set(local_sq)
    packed = gx_total(jnp.concatenate([rows_early, rows_late, extra], axis=0))
    squares = packed[-1, 0]
    half = rows_early.shape[0]
    rows_sum = jnp.stack([packed[:half], packed[half:2 * half]])
    power = squares / float(total_x * total_y * depth)
    grad_rows = rows_sum / jnp.sqrt(float(total_x) * (power + 1e-06))
    return (chi_start, grad_rows, jnp.reshape(power, (1,)))


def solution(mesh):
    placed = (
        P(None, ("starts", "gx"), "gy", None),
        P(None, ("starts", "gx"), "gy", None),
        P(None, ("starts", "gx"), "gy", None),
        P("gx", "gy", None),
        P("starts", "gy", None),
    )
    return jax.shard_map(
        on_device,
        mesh=mesh,
        in_specs=placed,
        out_specs=(P(None, ("starts", "gx"), "gy", None), P("starts", "gy", None), P("starts")),
        check_vma=False,
    )
```

```python
import math

import jax
import jax.numpy as jnp
from jax import lax
from jax.sharding import PartitionSpec as P

COUPLING = 1.0
STEP_SIZE = 0.2


def axis_sum(value, axis):
    count = lax.axis_size(axis)
    if count & (count - 1):
        return lax.psum(value, axis)
    step = 1
    while step < count:
        pairs = [(i, i ^ step) for i in range(count)]
        value = value + lax.ppermute(value, axis, pairs)
        step *= 2
    return value


def gx_total(value):
    count = lax.axis_size("gx")
    if count > 8 or count % 2:
        return axis_sum(value, "gx")
    pair = value + lax.ppermute(value, "gx", [(i, i ^ 1) for i in range(count)])
    groups = count // 2
    if groups == 1:
        return pair
    fetched = [pair] + [
        lax.ppermute(pair, "gx", [(i, i ^ (2 * k)) for i in range(count)])
        for k in range(1, groups)
    ]
    stacked = jnp.stack(fetched)
    mine = lax.axis_index("gx") // 2
    total = lax.dynamic_index_in_dim(stacked, mine, keepdims=False)
    for j in range(1, groups):
        total = total + lax.dynamic_index_in_dim(stacked, mine ^ j, keepdims=False)
    return total


def y_extended(block):
    ny = lax.axis_size("gy")
    iy = lax.axis_index("gy")
    Y = block.shape[2]
    if ny == 2:
        strip = lax.dynamic_slice_in_dim(block, (1 - iy) * (Y - 1), 1, axis=2)
        other = lax.ppermute(strip, "gy", [(0, 1), (1, 0)])
        zero = jnp.zeros_like(other)
        below = jnp.where(iy == 1, other, zero)
        above = jnp.where(iy == 0, other, zero)
    else:
        below = lax.ppermute(block[:, :, Y - 1:], "gy", [(j, j + 1) for j in range(ny - 1)])
        above = lax.ppermute(block[:, :, :1], "gy", [(j + 1, j) for j in range(ny - 1)])
    return jnp.concatenate([below, block, above], axis=2)


def coefficients(psi, trap, control, profile):
    real_part = psi[0]
    imag_part = psi[1]
    fine_control = jnp.repeat(control, 2, axis=0)
    potential = trap + profile[:, None, None] * fine_control[None, :, :]
    weight = potential + 2.0 * COUPLING * (real_part * real_part + imag_part * imag_part)
    mix_a = COUPLING * (real_part * real_part - imag_part * imag_part)
    mix_b = 2.0 * COUPLING * real_part * imag_part
    return (weight, mix_a, mix_b)


def apply_coef(lapl, field, coef):
    weight, mix_a, mix_b = coef
    real_part = field[0]
    imag_part = field[1]
    upper = -0.5 * lapl[0] + (weight + mix_a) * real_part + mix_b * imag_part
    lower = -0.5 * lapl[1] + mix_b * real_part + (weight - mix_a) * imag_part
    return jnp.stack([-lower, upper])


def operator(tall, x_low, x_high, coef):
    field = tall[:, :, 1:-1]
    x_padded = jnp.concatenate([x_low, field, x_high], axis=1)
    z_padded = jnp.pad(field, ((0, 0), (0, 0), (0, 0), (1, 1)))
    total = x_padded[:, 2:] + x_padded[:, :-2]
    total = total + tall[:, :, 2:] + tall[:, :, :-2]
    total = total + z_padded[:, :, :, 2:] + z_padded[:, :, :, :-2]
    lapl = total - 6.0 * field
    return apply_coef(lapl, field, coef)


def cut(coef, lo, hi):
    return tuple(c[lo:hi] for c in coef)


def across(plane):
    return jnp.stack([0.5 * plane[1], -0.5 * plane[0]])


def with_partner_row(block, row):
    iy = lax.axis_index("gy")
    zero = jnp.zeros_like(row)
    below = jnp.where(iy == 1, row, zero)
    above = jnp.where(iy == 0, row, zero)
    return jnp.concatenate([below, block, above], axis=2)


def edge_rows(block, offset=0):
    iy = lax.axis_index("gy")
    Y = block.shape[2]
    start = (1 - iy) * (Y - 1 - offset) + iy * offset
    return lax.dynamic_slice_in_dim(block, start, 1, axis=2)


def partner_coef(coef):
    rows = jnp.stack([edge_rows(c[:, None])[:, 0] for c in coef])
    got = lax.ppermute(rows, "gy", [(0, 1), (1, 0)])
    return tuple(got[k] for k in range(len(coef)))


def stage_pair(stage, base, base_low, base_high, coef, weight, tall=None, coef_partner=None):
    nx = lax.axis_size("gx")
    ix = lax.axis_index("gx")
    iy = lax.axis_index("gy")
    X = stage.shape[1]
    up = [(i, i + 1) for i in range(nx - 1)]
    down = [(i + 1, i) for i in range(nx - 1)]
    if tall is None:
        tall = y_extended(stage)
    zero_plane = jnp.zeros_like(stage[:, :1])
    part_top = operator(tall[:, X - 1:], stage[:, X - 2:X - 1], zero_plane, cut(coef, X - 1, X))
    part_bottom = operator(tall[:, :1], zero_plane, stage[:, 1:2], cut(coef, 0, 1))
    from_low = lax.ppermute(jnp.concatenate([stage[:, X - 1:], part_top]), "gx", up)
    from_high = lax.ppermute(jnp.concatenate([stage[:, :1], part_bottom]), "gx", down)
    stage_low, part_low = from_low[:2], from_low[2:]
    stage_high, part_high = from_high[:2], from_high[2:]
    if base_low is None:
        base_low, base_high = stage_low, stage_high
    section = operator(tall, stage_low, stage_high, coef)
    section_low = part_low + across(stage[:, :1])
    section_high = part_high + across(stage[:, X - 1:])
    nxt = base + weight * section
    nxt_low = jnp.where(ix > 0, base_low + weight * section_low, 0.0)
    nxt_high = jnp.where(ix < nx - 1, base_high + weight * section_high, 0.0)
    if coef_partner is None:
        section_next = operator(y_extended(nxt), nxt_low, nxt_high, coef)
        return section, section_next, base_low, base_high, None
    mine_stage = edge_rows(stage)
    mine = edge_rows(nxt)
    pack = jnp.concatenate(
        [mine, edge_rows(nxt, 1), edge_rows(nxt_low), edge_rows(nxt_high),
         edge_rows(stage, 1), edge_rows(stage_low), edge_rows(stage_high)],
        axis=1,
    )
    got = lax.ppermute(pack, "gy", [(0, 1), (1, 0)])
    their, their_inner = got[:, :X], got[:, X:2 * X]
    their_low, their_high = got[:, 2 * X:2 * X + 1], got[:, 2 * X + 1:2 * X + 2]
    their_stage_inner = got[:, 2 * X + 2:3 * X + 2]
    their_stage_low, their_stage_high = got[:, 3 * X + 2:3 * X + 3], got[:, 3 * X + 3:3 * X + 4]
    section_next = operator(with_partner_row(nxt, their), nxt_low, nxt_high, coef)

    def beside(mine_row, their_row, their_inner_row):
        return jnp.where(
            iy == 0,
            jnp.concatenate([mine_row, their_row, their_inner_row], axis=2),
            jnp.concatenate([their_inner_row, their_row, mine_row], axis=2),
        )

    their_stage = jnp.where(iy == 1, tall[:, :, :1], tall[:, :, -1:])
    their_section = operator(
        beside(mine_stage, their_stage, their_stage_inner), their_stage_low, their_stage_high,
        coef_partner,
    )
    their_section_next = operator(beside(mine, their, their_inner), their_low, their_high, coef_partner)
    return section, section_next, base_low, base_high, (their_stage, their_section, their_section_next)


def rk_step(field, coef, tall=None):
    fast = lax.axis_size("gy") == 2 and field.shape[2] >= 3
    partner = partner_coef(coef) if fast else None
    section_one, section_two, low, high, first = stage_pair(
        field, field, None, None, coef, 0.5 * STEP_SIZE, tall=tall, coef_partner=partner
    )
    stage_three = field + 0.5 * STEP_SIZE * section_two
    tall_three = None
    if fast:
        their_field, their_one, their_two = first
        their_three = their_field + 0.5 * STEP_SIZE * their_two
        tall_three = with_partner_row(stage_three, their_three)
    section_three, section_four, _, _, second = stage_pair(
        stage_three, field, low, high, coef, STEP_SIZE, tall=tall_three, coef_partner=partner
    )
    result = field + STEP_SIZE / 6.0 * (
        section_one + 2.0 * section_two + 2.0 * section_three + section_four
    )
    if not fast:
        return result, None
    _, their_three_section, their_four = second
    their_result = their_field + STEP_SIZE / 6.0 * (
        their_one + 2.0 * their_two + 2.0 * their_three_section + their_four
    )
    return result, with_partner_row(result, their_result)


def row_terms(field, psi, profile):
    intersection = field[0] * psi[1] - field[1] * psi[0]
    summed = jnp.sum(intersection * profile[:, None, None], axis=0)
    return summed.reshape(summed.shape[0] // 2, 2, summed.shape[1]).sum(axis=1)


def on_device(chi_final, psi_late, psi_early, trap, controls):
    planes = chi_final.shape[1]
    width_y = chi_final.shape[2]
    depth = chi_final.shape[3]
    total_x = planes * lax.axis_size("gx")
    total_y = width_y * lax.axis_size("gy")
    first = lax.axis_index("gx") * planes
    x_index = (first + jnp.arange(planes, dtype=jnp.int32)).astype(jnp.float32)
    profile = 1.0 + 0.5 * jnp.cos(2.0 * math.pi * x_index / float(total_x))
    coef_late = coefficients(psi_late, trap, controls[1], profile)
    coef_early = coefficients(psi_early, trap, controls[0], profile)
    chi_late, tall_late = rk_step(chi_final, coef_late)
    chi_start, _ = rk_step(chi_late, coef_early, tall=tall_late)
    rows_late = row_terms(chi_late, psi_late, profile)
    rows_early = row_terms(chi_start, psi_early, profile)
    local_sq = axis_sum(jnp.sum(chi_start * chi_start), "gy")
    extra = jnp.zeros((1, rows_early.shape[1]), jnp.float32).at[0, 0].set(local_sq)
    packed = gx_total(jnp.concatenate([rows_early, rows_late, extra], axis=0))
    squares = packed[-1, 0]
    half = rows_early.shape[0]
    rows_sum = jnp.stack([packed[:half], packed[half:2 * half]])
    power = squares / float(total_x * total_y * depth)
    grad_rows = rows_sum / jnp.sqrt(float(total_x) * (power + 1e-06))
    return (chi_start, grad_rows, jnp.reshape(power, (1,)))


def solution(mesh):
    placed = (
        P(None, ("starts", "gx"), "gy", None),
        P(None, ("starts", "gx"), "gy", None),
        P(None, ("starts", "gx"), "gy", None),
        P("gx", "gy", None),
        P("starts", "gy", None),
    )
    return jax.shard_map(
        on_device,
        mesh=mesh,
        in_specs=placed,
        out_specs=(P(None, ("starts", "gx"), "gy", None), P("starts", "gy", None), P("starts")),
        check_vma=False,
    )
```

```python
import math

import jax
import jax.numpy as jnp
from jax import lax
from jax.sharding import PartitionSpec as P

COUPLING = 1.0
STEP_SIZE = 0.2


def axis_sum(value, axis):
    count = lax.axis_size(axis)
    if count & (count - 1):
        return lax.psum(value, axis)
    step = 1
    while step < count:
        pairs = [(i, i ^ step) for i in range(count)]
        value = value + lax.ppermute(value, axis, pairs)
        step *= 2
    return value


def gx_total(value):
    count = lax.axis_size("gx")
    if count > 8 or count % 2:
        return axis_sum(value, "gx")
    pair = value + lax.ppermute(value, "gx", [(i, i ^ 1) for i in range(count)])
    groups = count // 2
    if groups == 1:
        return pair
    fetched = [pair] + [
        lax.ppermute(pair, "gx", [(i, i ^ (2 * k)) for i in range(count)])
        for k in range(1, groups)
    ]
    stacked = jnp.stack(fetched)
    mine = lax.axis_index("gx") // 2
    total = lax.dynamic_index_in_dim(stacked, mine, keepdims=False)
    for j in range(1, groups):
        total = total + lax.dynamic_index_in_dim(stacked, mine ^ j, keepdims=False)
    return total


def y_extended(block):
    ny = lax.axis_size("gy")
    iy = lax.axis_index("gy")
    Y = block.shape[2]
    if ny == 2:
        strip = lax.dynamic_slice_in_dim(block, (1 - iy) * (Y - 1), 1, axis=2)
        other = lax.ppermute(strip, "gy", [(0, 1), (1, 0)])
        zero = jnp.zeros_like(other)
        below = jnp.where(iy == 1, other, zero)
        above = jnp.where(iy == 0, other, zero)
    else:
        below = lax.ppermute(block[:, :, Y - 1:], "gy", [(j, j + 1) for j in range(ny - 1)])
        above = lax.ppermute(block[:, :, :1], "gy", [(j + 1, j) for j in range(ny - 1)])
    return jnp.concatenate([below, block, above], axis=2)


def coefficients(psi, trap, control, profile):
    real_part = psi[0]
    imag_part = psi[1]
    fine_control = jnp.repeat(control, 2, axis=0)
    potential = trap + profile[:, None, None] * fine_control[None, :, :]
    weight = potential + 2.0 * COUPLING * (real_part * real_part + imag_part * imag_part)
    mix_a = COUPLING * (real_part * real_part - imag_part * imag_part)
    mix_b = 2.0 * COUPLING * real_part * imag_part
    return (weight, mix_a, mix_b)


def apply_coef(lapl, field, coef):
    weight, mix_a, mix_b = coef
    real_part = field[0]
    imag_part = field[1]
    upper = -0.5 * lapl[0] + (weight + mix_a) * real_part + mix_b * imag_part
    lower = -0.5 * lapl[1] + mix_b * real_part + (weight - mix_a) * imag_part
    return jnp.stack([-lower, upper])


def operator(tall, x_low, x_high, coef):
    field = tall[:, :, 1:-1]
    x_padded = jnp.concatenate([x_low, field, x_high], axis=1)
    z_padded = jnp.pad(field, ((0, 0), (0, 0), (0, 0), (1, 1)))
    total = x_padded[:, 2:] + x_padded[:, :-2]
    total = total + tall[:, :, 2:] + tall[:, :, :-2]
    total = total + z_padded[:, :, :, 2:] + z_padded[:, :, :, :-2]
    lapl = total - 6.0 * field
    return apply_coef(lapl, field, coef)


def cut(coef, lo, hi):
    return tuple(c[lo:hi] for c in coef)


def across(plane):
    return jnp.stack([0.5 * plane[1], -0.5 * plane[0]])


def with_partner_row(block, row):
    iy = lax.axis_index("gy")
    zero = jnp.zeros_like(row)
    below = jnp.where(iy == 1, row, zero)
    above = jnp.where(iy == 0, row, zero)
    return jnp.concatenate([below, block, above], axis=2)


def edge_rows(block, offset=0):
    iy = lax.axis_index("gy")
    Y = block.shape[2]
    start = (1 - iy) * (Y - 1 - offset) + iy * offset
    return lax.dynamic_slice_in_dim(block, start, 1, axis=2)


def partner_coef(coef):
    rows = jnp.stack([edge_rows(c[:, None])[:, 0] for c in coef])
    got = lax.ppermute(rows, "gy", [(0, 1), (1, 0)])
    return tuple(got[k] for k in range(len(coef)))


def stage_pair(stage, base, base_low, base_high, coef, weight, tall=None, ahead=None):
    nx = lax.axis_size("gx")
    ix = lax.axis_index("gx")
    iy = lax.axis_index("gy")
    X = stage.shape[1]
    up = [(i, i + 1) for i in range(nx - 1)]
    down = [(i + 1, i) for i in range(nx - 1)]
    late_y = tall is None and ahead is not None
    if tall is None:
        tall = y_extended(stage)
    send_tall = zero_extended(stage) if late_y else tall
    zero_plane = jnp.zeros_like(stage[:, :1])
    part_top = operator(send_tall[:, X - 1:], stage[:, X - 2:X - 1], zero_plane, cut(coef, X - 1, X))
    part_bottom = operator(send_tall[:, :1], zero_plane, stage[:, 1:2], cut(coef, 0, 1))
    from_low = lax.ppermute(jnp.concatenate([stage[:, X - 1:], part_top]), "gx", up)
    from_high = lax.ppermute(jnp.concatenate([stage[:, :1], part_bottom]), "gx", down)
    stage_low, part_low = from_low[:2], from_low[2:]
    stage_high, part_high = from_high[:2], from_high[2:]
    if base_low is None:
        base_low, base_high = stage_low, stage_high
    section = operator(tall, stage_low, stage_high, coef)
    section_low = part_low + across(stage[:, :1])
    section_high = part_high + across(stage[:, X - 1:])
    nxt = base + weight * section
    nxt_low = jnp.where(ix > 0, base_low + weight * section_low, 0.0)
    nxt_high = jnp.where(ix < nx - 1, base_high + weight * section_high, 0.0)
    if ahead is None:
        section_next = operator(y_extended(nxt), nxt_low, nxt_high, coef)
        return section, section_next, base_low, base_high, None
    next_weight, coef_partner = ahead
    Y = stage.shape[2]
    edge = (1 - iy) * (Y - 1)
    mine = edge_rows(nxt)
    pack = jnp.concatenate(
        [mine, edge_rows(nxt, 1), edge_rows(stage_low), edge_rows(stage_high),
         edge_rows(section_low), edge_rows(section_high)],
        axis=1,
    )
    got = lax.ppermute(pack, "gy", [(0, 1), (1, 0)])
    their, their_inner = got[:, :X], got[:, X:2 * X]
    t_stage_low, t_stage_high, t_low, t_high = (
        got[:, 2 * X + k:2 * X + k + 1] for k in range(4)
    )

    def halo_edge(part, base_x, other, keep):
        return jnp.where(keep, base_x + weight * (part + across(other)), 0.0)

    if late_y:
        nxt_low = lax.dynamic_update_slice_in_dim(
            nxt_low,
            halo_edge(edge_rows(section_low), edge_rows(base_low), t_stage_low, ix > 0),
            edge, axis=2,
        )
        nxt_high = lax.dynamic_update_slice_in_dim(
            nxt_high,
            halo_edge(edge_rows(section_high), edge_rows(base_high), t_stage_high, ix < nx - 1),
            edge, axis=2,
        )
        their_low = halo_edge(t_low, t_stage_low, edge_rows(stage_low), ix > 0)
        their_high = halo_edge(t_high, t_stage_high, edge_rows(stage_high), ix < nx - 1)
    else:
        their_low = jnp.where(ix > 0, t_stage_low + weight * t_low, 0.0)
        their_high = jnp.where(ix < nx - 1, t_stage_high + weight * t_high, 0.0)
    section_next = operator(with_partner_row(nxt, their), nxt_low, nxt_high, coef)
    slab = jnp.where(
        iy == 0,
        jnp.concatenate([mine, their, their_inner], axis=2),
        jnp.concatenate([their_inner, their, mine], axis=2),
    )
    their_section = operator(slab, their_low, their_high, coef_partner)
    their_base = jnp.where(iy == 1, tall[:, :, :1], tall[:, :, -1:])
    their_next = their_base + next_weight * their_section
    return section, section_next, base_low, base_high, their_next


def zero_extended(block):
    zero = jnp.zeros_like(block[:, :, :1])
    return jnp.concatenate([zero, block, zero], axis=2)


def rk_step(field, coef):
    fast = lax.axis_size("gy") == 2 and field.shape[2] >= 3
    ahead = (0.5 * STEP_SIZE, partner_coef(coef)) if fast else None
    section_one, section_two, low, high, their_three = stage_pair(
        field, field, None, None, coef, 0.5 * STEP_SIZE, ahead=ahead
    )
    stage_three = field + 0.5 * STEP_SIZE * section_two
    tall_three = with_partner_row(stage_three, their_three) if fast else None
    section_three, section_four, _, _, _ = stage_pair(
        stage_three, field, low, high, coef, STEP_SIZE, tall=tall_three
    )
    return field + STEP_SIZE / 6.0 * (
        section_one + 2.0 * section_two + 2.0 * section_three + section_four
    )


def row_terms(field, psi, profile):
    intersection = field[0] * psi[1] - field[1] * psi[0]
    summed = jnp.sum(intersection * profile[:, None, None], axis=0)
    return summed.reshape(summed.shape[0] // 2, 2, summed.shape[1]).sum(axis=1)


def on_device(chi_final, psi_late, psi_early, trap, controls):
    planes = chi_final.shape[1]
    width_y = chi_final.shape[2]
    depth = chi_final.shape[3]
    total_x = planes * lax.axis_size("gx")
    total_y = width_y * lax.axis_size("gy")
    first = lax.axis_index("gx") * planes
    x_index = (first + jnp.arange(planes, dtype=jnp.int32)).astype(jnp.float32)
    profile = 1.0 + 0.5 * jnp.cos(2.0 * math.pi * x_index / float(total_x))
    coef_late = coefficients(psi_late, trap, controls[1], profile)
    coef_early = coefficients(psi_early, trap, controls[0], profile)
    chi_late = rk_step(chi_final, coef_late)
    chi_start = rk_step(chi_late, coef_early)
    rows_late = row_terms(chi_late, psi_late, profile)
    rows_early = row_terms(chi_start, psi_early, profile)
    local_sq = axis_sum(jnp.sum(chi_start * chi_start), "gy")
    extra = jnp.zeros((1, rows_early.shape[1]), jnp.float32).at[0, 0].set(local_sq)
    packed = gx_total(jnp.concatenate([rows_early, rows_late, extra], axis=0))
    squares = packed[-1, 0]
    half = rows_early.shape[0]
    rows_sum = jnp.stack([packed[:half], packed[half:2 * half]])
    power = squares / float(total_x * total_y * depth)
    grad_rows = rows_sum / jnp.sqrt(float(total_x) * (power + 1e-06))
    return (chi_start, grad_rows, jnp.reshape(power, (1,)))


def solution(mesh):
    placed = (
        P(None, ("starts", "gx"), "gy", None),
        P(None, ("starts", "gx"), "gy", None),
        P(None, ("starts", "gx"), "gy", None),
        P("gx", "gy", None),
        P("starts", "gy", None),
    )
    return jax.shard_map(
        on_device,
        mesh=mesh,
        in_specs=placed,
        out_specs=(P(None, ("starts", "gx"), "gy", None), P("starts", "gy", None), P("starts")),
        check_vma=False,
    )
```

```python
import math

import jax
import jax.numpy as jnp
from jax import lax
from jax.sharding import PartitionSpec as P

COUPLING = 1.0
STEP_SIZE = 0.2


def axis_sum(value, axis):
    count = lax.axis_size(axis)
    if count & (count - 1):
        return lax.psum(value, axis)
    step = 1
    while step < count:
        pairs = [(i, i ^ step) for i in range(count)]
        value = value + lax.ppermute(value, axis, pairs)
        step *= 2
    return value


def gx_total(value):
    count = lax.axis_size("gx")
    if count > 8 or count % 2:
        return axis_sum(value, "gx")
    pair = value + lax.ppermute(value, "gx", [(i, i ^ 1) for i in range(count)])
    groups = count // 2
    if groups == 1:
        return pair
    fetched = [pair] + [
        lax.ppermute(pair, "gx", [(i, i ^ (2 * k)) for i in range(count)])
        for k in range(1, groups)
    ]
    stacked = jnp.stack(fetched)
    mine = lax.axis_index("gx") // 2
    total = lax.dynamic_index_in_dim(stacked, mine, keepdims=False)
    for j in range(1, groups):
        total = total + lax.dynamic_index_in_dim(stacked, mine ^ j, keepdims=False)
    return total


def y_extended(block):
    ny = lax.axis_size("gy")
    iy = lax.axis_index("gy")
    Y = block.shape[2]
    if ny == 2:
        strip = lax.dynamic_slice_in_dim(block, (1 - iy) * (Y - 1), 1, axis=2)
        other = lax.ppermute(strip, "gy", [(0, 1), (1, 0)])
        zero = jnp.zeros_like(other)
        below = jnp.where(iy == 1, other, zero)
        above = jnp.where(iy == 0, other, zero)
    else:
        below = lax.ppermute(block[:, :, Y - 1:], "gy", [(j, j + 1) for j in range(ny - 1)])
        above = lax.ppermute(block[:, :, :1], "gy", [(j + 1, j) for j in range(ny - 1)])
    return jnp.concatenate([below, block, above], axis=2)


def coefficients(psi, trap, control, profile):
    real_part = psi[0]
    imag_part = psi[1]
    fine_control = jnp.repeat(control, 2, axis=0)
    potential = trap + profile[:, None, None] * fine_control[None, :, :]
    weight = potential + 2.0 * COUPLING * (real_part * real_part + imag_part * imag_part)
    mix_a = COUPLING * (real_part * real_part - imag_part * imag_part)
    mix_b = 2.0 * COUPLING * real_part * imag_part
    return (weight, mix_a, mix_b)


def apply_coef(lapl, field, coef):
    weight, mix_a, mix_b = coef
    real_part = field[0]
    imag_part = field[1]
    upper = -0.5 * lapl[0] + (weight + mix_a) * real_part + mix_b * imag_part
    lower = -0.5 * lapl[1] + mix_b * real_part + (weight - mix_a) * imag_part
    return jnp.stack([-lower, upper])


def operator(tall, x_low, x_high, coef):
    field = tall[:, :, 1:-1]
    x_padded = jnp.concatenate([x_low, field, x_high], axis=1)
    z_padded = jnp.pad(field, ((0, 0), (0, 0), (0, 0), (1, 1)))
    total = x_padded[:, 2:] + x_padded[:, :-2]
    total = total + tall[:, :, 2:] + tall[:, :, :-2]
    total = total + z_padded[:, :, :, 2:] + z_padded[:, :, :, :-2]
    lapl = total - 6.0 * field
    return apply_coef(lapl, field, coef)


def cut(coef, lo, hi):
    return tuple(c[lo:hi] for c in coef)


def across(plane):
    return jnp.stack([0.5 * plane[1], -0.5 * plane[0]])


def with_partner_row(block, row):
    iy = lax.axis_index("gy")
    zero = jnp.zeros_like(row)
    below = jnp.where(iy == 1, row, zero)
    above = jnp.where(iy == 0, row, zero)
    return jnp.concatenate([below, block, above], axis=2)


def edge_rows(block, offset=0):
    iy = lax.axis_index("gy")
    Y = block.shape[2]
    start = (1 - iy) * (Y - 1 - offset) + iy * offset
    return lax.dynamic_slice_in_dim(block, start, 1, axis=2)


def partner_coef(coef):
    rows = jnp.stack([edge_rows(c[:, None])[:, 0] for c in coef])
    got = lax.ppermute(rows, "gy", [(0, 1), (1, 0)])
    return tuple(got[k] for k in range(len(coef)))


def stage_pair(stage, base, base_low, base_high, coef, weight, tall=None, ahead=None, edge_coef=None):
    nx = lax.axis_size("gx")
    ix = lax.axis_index("gx")
    iy = lax.axis_index("gy")
    X = stage.shape[1]
    up = [(i, i + 1) for i in range(nx - 1)]
    down = [(i + 1, i) for i in range(nx - 1)]
    if tall is None:
        tall = y_extended(stage)
    zero_plane = jnp.zeros_like(stage[:, :1])
    coef_top, coef_bottom = edge_coef or (cut(coef, X - 1, X), cut(coef, 0, 1))
    part_top = operator(tall[:, X - 1:], stage[:, X - 2:X - 1], zero_plane, coef_top)
    part_bottom = operator(tall[:, :1], zero_plane, stage[:, 1:2], coef_bottom)
    from_low = lax.ppermute(jnp.concatenate([stage[:, X - 1:], part_top]), "gx", up)
    from_high = lax.ppermute(jnp.concatenate([stage[:, :1], part_bottom]), "gx", down)
    stage_low, part_low = from_low[:2], from_low[2:]
    stage_high, part_high = from_high[:2], from_high[2:]
    if base_low is None:
        base_low, base_high = stage_low, stage_high
    section = operator(tall, stage_low, stage_high, coef)
    section_low = part_low + across(stage[:, :1])
    section_high = part_high + across(stage[:, X - 1:])
    nxt = base + weight * section
    nxt_low = jnp.where(ix > 0, base_low + weight * section_low, 0.0)
    nxt_high = jnp.where(ix < nx - 1, base_high + weight * section_high, 0.0)
    if ahead is None:
        section_next = operator(y_extended(nxt), nxt_low, nxt_high, coef)
        return section, section_next, base_low, base_high, None
    next_weight, coef_partner = ahead
    mine = edge_rows(nxt)
    pack = jnp.concatenate(
        [mine, edge_rows(nxt, 1), edge_rows(nxt_low), edge_rows(nxt_high)], axis=1
    )
    got = lax.ppermute(pack, "gy", [(0, 1), (1, 0)])
    their, their_inner = got[:, :X], got[:, X:2 * X]
    their_low, their_high = got[:, 2 * X:2 * X + 1], got[:, 2 * X + 1:2 * X + 2]
    section_next = operator(with_partner_row(nxt, their), nxt_low, nxt_high, coef)
    slab = jnp.where(
        iy == 0,
        jnp.concatenate([mine, their, their_inner], axis=2),
        jnp.concatenate([their_inner, their, mine], axis=2),
    )
    their_section = operator(slab, their_low, their_high, coef_partner)
    their_base = jnp.where(iy == 1, tall[:, :, :1], tall[:, :, -1:])
    their_next = their_base + next_weight * their_section
    return section, section_next, base_low, base_high, their_next


def rk_step(field, coef, edge_coef=None):
    fast = lax.axis_size("gy") == 2 and field.shape[2] >= 3
    ahead = (0.5 * STEP_SIZE, partner_coef(coef)) if fast else None
    section_one, section_two, low, high, their_three = stage_pair(
        field, field, None, None, coef, 0.5 * STEP_SIZE, ahead=ahead, edge_coef=edge_coef
    )
    stage_three = field + 0.5 * STEP_SIZE * section_two
    tall_three = with_partner_row(stage_three, their_three) if fast else None
    section_three, section_four, _, _, _ = stage_pair(
        stage_three, field, low, high, coef, STEP_SIZE, tall=tall_three
    )
    return field + STEP_SIZE / 6.0 * (
        section_one + 2.0 * section_two + 2.0 * section_three + section_four
    )


def row_terms(field, psi, profile):
    intersection = field[0] * psi[1] - field[1] * psi[0]
    summed = jnp.sum(intersection * profile[:, None, None], axis=0)
    return summed.reshape(summed.shape[0] // 2, 2, summed.shape[1]).sum(axis=1)


def on_device(chi_final, psi_late, psi_early, trap, controls):
    planes = chi_final.shape[1]
    width_y = chi_final.shape[2]
    depth = chi_final.shape[3]
    total_x = planes * lax.axis_size("gx")
    total_y = width_y * lax.axis_size("gy")
    first = lax.axis_index("gx") * planes
    x_index = (first + jnp.arange(planes, dtype=jnp.int32)).astype(jnp.float32)
    profile = 1.0 + 0.5 * jnp.cos(2.0 * math.pi * x_index / float(total_x))
    coef_late = coefficients(psi_late, trap, controls[1], profile)
    coef_early = coefficients(psi_early, trap, controls[0], profile)
    edge_late = (
        coefficients(psi_late[:, planes - 1:], trap[planes - 1:], controls[1], profile[planes - 1:]),
        coefficients(psi_late[:, :1], trap[:1], controls[1], profile[:1]),
    )
    chi_late = rk_step(chi_final, coef_late, edge_late)
    chi_start = rk_step(chi_late, coef_early)
    rows_late = row_terms(chi_late, psi_late, profile)
    rows_early = row_terms(chi_start, psi_early, profile)
    local_sq = axis_sum(jnp.sum(chi_start * chi_start), "gy")
    extra = jnp.zeros((1, rows_early.shape[1]), jnp.float32).at[0, 0].set(local_sq)
    packed = gx_total(jnp.concatenate([rows_early, rows_late, extra], axis=0))
    squares = packed[-1, 0]
    half = rows_early.shape[0]
    rows_sum = jnp.stack([packed[:half], packed[half:2 * half]])
    power = squares / float(total_x * total_y * depth)
    grad_rows = rows_sum / jnp.sqrt(float(total_x) * (power + 1e-06))
    return (chi_start, grad_rows, jnp.reshape(power, (1,)))


def solution(mesh):
    placed = (
        P(None, ("starts", "gx"), "gy", None),
        P(None, ("starts", "gx"), "gy", None),
        P(None, ("starts", "gx"), "gy", None),
        P("gx", "gy", None),
        P("starts", "gy", None),
    )
    return jax.shard_map(
        on_device,
        mesh=mesh,
        in_specs=placed,
        out_specs=(P(None, ("starts", "gx"), "gy", None), P("starts", "gy", None), P("starts")),
        check_vma=False,
    )
```

```python
import math

import jax
import jax.numpy as jnp
from jax import lax
from jax.sharding import PartitionSpec as P

COUPLING = 1.0
STEP_SIZE = 0.2


def axis_sum(value, axis):
    count = lax.axis_size(axis)
    if count & (count - 1):
        return lax.psum(value, axis)
    step = 1
    while step < count:
        pairs = [(i, i ^ step) for i in range(count)]
        value = value + lax.ppermute(value, axis, pairs)
        step *= 2
    return value


def gx_total(value, square=None):
    count = lax.axis_size("gx")
    if count > 8 or count % 2 or (square is not None and lax.axis_size("gy") != 2):
        if square is not None:
            value = value.at[-1, 0].set(axis_sum(square, "gy"))
        return axis_sum(value, "gx")
    pair = value + lax.ppermute(value, "gx", [(i, i ^ 1) for i in range(count)])
    if square is not None:
        ny = lax.axis_size("gy")
        other = lax.ppermute(square, "gy", [(0, 1), (1, 0)])
        across_pair = lax.ppermute(
            square, ("gx", "gy"),
            [(i * ny + j, (i ^ 1) * ny + (1 - j)) for i in range(count) for j in range(ny)],
        )
        group = pair[-1, 0] + (other + across_pair)
        pair = pair.at[-1, 0].set(group)
    groups = count // 2
    if groups == 1:
        return pair
    fetched = [pair] + [
        lax.ppermute(pair, "gx", [(i, i ^ (2 * k)) for i in range(count)])
        for k in range(1, groups)
    ]
    stacked = jnp.stack(fetched)
    mine = lax.axis_index("gx") // 2
    total = lax.dynamic_index_in_dim(stacked, mine, keepdims=False)
    for j in range(1, groups):
        total = total + lax.dynamic_index_in_dim(stacked, mine ^ j, keepdims=False)
    return total


def y_extended(block):
    ny = lax.axis_size("gy")
    iy = lax.axis_index("gy")
    Y = block.shape[2]
    if ny == 2:
        strip = lax.dynamic_slice_in_dim(block, (1 - iy) * (Y - 1), 1, axis=2)
        other = lax.ppermute(strip, "gy", [(0, 1), (1, 0)])
        zero = jnp.zeros_like(other)
        below = jnp.where(iy == 1, other, zero)
        above = jnp.where(iy == 0, other, zero)
    else:
        below = lax.ppermute(block[:, :, Y - 1:], "gy", [(j, j + 1) for j in range(ny - 1)])
        above = lax.ppermute(block[:, :, :1], "gy", [(j + 1, j) for j in range(ny - 1)])
    return jnp.concatenate([below, block, above], axis=2)


def coefficients(psi, trap, control, profile):
    real_part = psi[0]
    imag_part = psi[1]
    fine_control = jnp.repeat(control, 2, axis=0)
    potential = trap + profile[:, None, None] * fine_control[None, :, :]
    weight = potential + 2.0 * COUPLING * (real_part * real_part + imag_part * imag_part)
    mix_a = COUPLING * (real_part * real_part - imag_part * imag_part)
    mix_b = 2.0 * COUPLING * real_part * imag_part
    return (weight, mix_a, mix_b)


def apply_coef(lapl, field, coef):
    weight, mix_a, mix_b = coef
    real_part = field[0]
    imag_part = field[1]
    upper = -0.5 * lapl[0] + (weight + mix_a) * real_part + mix_b * imag_part
    lower = -0.5 * lapl[1] + mix_b * real_part + (weight - mix_a) * imag_part
    return jnp.stack([-lower, upper])


def operator(tall, x_low, x_high, coef):
    field = tall[:, :, 1:-1]
    x_padded = jnp.concatenate([x_low, field, x_high], axis=1)
    z_padded = jnp.pad(field, ((0, 0), (0, 0), (0, 0), (1, 1)))
    total = x_padded[:, 2:] + x_padded[:, :-2]
    total = total + tall[:, :, 2:] + tall[:, :, :-2]
    total = total + z_padded[:, :, :, 2:] + z_padded[:, :, :, :-2]
    lapl = total - 6.0 * field
    return apply_coef(lapl, field, coef)


def cut(coef, lo, hi):
    return tuple(c[lo:hi] for c in coef)


def across(plane):
    return jnp.stack([0.5 * plane[1], -0.5 * plane[0]])


def with_partner_row(block, row):
    iy = lax.axis_index("gy")
    zero = jnp.zeros_like(row)
    below = jnp.where(iy == 1, row, zero)
    above = jnp.where(iy == 0, row, zero)
    return jnp.concatenate([below, block, above], axis=2)


def edge_rows(block, offset=0):
    iy = lax.axis_index("gy")
    Y = block.shape[2]
    start = (1 - iy) * (Y - 1 - offset) + iy * offset
    return lax.dynamic_slice_in_dim(block, start, 1, axis=2)


def partner_coef(coef):
    rows = jnp.stack([edge_rows(c[:, None])[:, 0] for c in coef])
    got = lax.ppermute(rows, "gy", [(0, 1), (1, 0)])
    return tuple(got[k] for k in range(len(coef)))


def stage_pair(stage, base, base_low, base_high, coef, weight, tall=None, ahead=None):
    nx = lax.axis_size("gx")
    ix = lax.axis_index("gx")
    iy = lax.axis_index("gy")
    X = stage.shape[1]
    up = [(i, i + 1) for i in range(nx - 1)]
    down = [(i + 1, i) for i in range(nx - 1)]
    if tall is None:
        tall = y_extended(stage)
    zero_plane = jnp.zeros_like(stage[:, :1])
    part_top = operator(tall[:, X - 1:], stage[:, X - 2:X - 1], zero_plane, cut(coef, X - 1, X))
    part_bottom = operator(tall[:, :1], zero_plane, stage[:, 1:2], cut(coef, 0, 1))
    from_low = lax.ppermute(jnp.concatenate([stage[:, X - 1:], part_top]), "gx", up)
    from_high = lax.ppermute(jnp.concatenate([stage[:, :1], part_bottom]), "gx", down)
    stage_low, part_low = from_low[:2], from_low[2:]
    stage_high, part_high = from_high[:2], from_high[2:]
    if base_low is None:
        base_low, base_high = stage_low, stage_high
    section = operator(tall, stage_low, stage_high, coef)
    section_low = part_low + across(stage[:, :1])
    section_high = part_high + across(stage[:, X - 1:])
    nxt = base + weight * section
    nxt_low = jnp.where(ix > 0, base_low + weight * section_low, 0.0)
    nxt_high = jnp.where(ix < nx - 1, base_high + weight * section_high, 0.0)
    if ahead is None:
        section_next = operator(y_extended(nxt), nxt_low, nxt_high, coef)
        return section, section_next, base_low, base_high, None
    next_weight, coef_partner = ahead
    mine = edge_rows(nxt)
    pack = jnp.concatenate(
        [mine, edge_rows(nxt, 1), edge_rows(nxt_low), edge_rows(nxt_high)], axis=1
    )
    got = lax.ppermute(pack, "gy", [(0, 1), (1, 0)])
    their, their_inner = got[:, :X], got[:, X:2 * X]
    their_low, their_high = got[:, 2 * X:2 * X + 1], got[:, 2 * X + 1:2 * X + 2]
    section_next = operator(with_partner_row(nxt, their), nxt_low, nxt_high, coef)
    slab = jnp.where(
        iy == 0,
        jnp.concatenate([mine, their, their_inner], axis=2),
        jnp.concatenate([their_inner, their, mine], axis=2),
    )
    their_section = operator(slab, their_low, their_high, coef_partner)
    their_base = jnp.where(iy == 1, tall[:, :, :1], tall[:, :, -1:])
    their_next = their_base + next_weight * their_section
    return section, section_next, base_low, base_high, their_next


def rk_step(field, coef):
    fast = lax.axis_size("gy") == 2 and field.shape[2] >= 3
    ahead = (0.5 * STEP_SIZE, partner_coef(coef)) if fast else None
    section_one, section_two, low, high, their_three = stage_pair(
        field, field, None, None, coef, 0.5 * STEP_SIZE, ahead=ahead
    )
    stage_three = field + 0.5 * STEP_SIZE * section_two
    tall_three = with_partner_row(stage_three, their_three) if fast else None
    section_three, section_four, _, _, _ = stage_pair(
        stage_three, field, low, high, coef, STEP_SIZE, tall=tall_three
    )
    return field + STEP_SIZE / 6.0 * (
        section_one + 2.0 * section_two + 2.0 * section_three + section_four
    )


def row_terms(field, psi, profile):
    intersection = field[0] * psi[1] - field[1] * psi[0]
    summed = jnp.sum(intersection * profile[:, None, None], axis=0)
    return summed.reshape(summed.shape[0] // 2, 2, summed.shape[1]).sum(axis=1)


def on_device(chi_final, psi_late, psi_early, trap, controls):
    planes = chi_final.shape[1]
    width_y = chi_final.shape[2]
    depth = chi_final.shape[3]
    total_x = planes * lax.axis_size("gx")
    total_y = width_y * lax.axis_size("gy")
    first = lax.axis_index("gx") * planes
    x_index = (first + jnp.arange(planes, dtype=jnp.int32)).astype(jnp.float32)
    profile = 1.0 + 0.5 * jnp.cos(2.0 * math.pi * x_index / float(total_x))
    coef_late = coefficients(psi_late, trap, controls[1], profile)
    coef_early = coefficients(psi_early, trap, controls[0], profile)
    chi_late = rk_step(chi_final, coef_late)
    chi_start = rk_step(chi_late, coef_early)
    rows_late = row_terms(chi_late, psi_late, profile)
    rows_early = row_terms(chi_start, psi_early, profile)
    local_sq = jnp.sum(chi_start * chi_start)
    extra = jnp.zeros((1, rows_early.shape[1]), jnp.float32).at[0, 0].set(local_sq)
    packed = gx_total(jnp.concatenate([rows_early, rows_late, extra], axis=0), local_sq)
    squares = packed[-1, 0]
    half = rows_early.shape[0]
    rows_sum = jnp.stack([packed[:half], packed[half:2 * half]])
    power = squares / float(total_x * total_y * depth)
    grad_rows = rows_sum / jnp.sqrt(float(total_x) * (power + 1e-06))
    return (chi_start, grad_rows, jnp.reshape(power, (1,)))


def solution(mesh):
    placed = (
        P(None, ("starts", "gx"), "gy", None),
        P(None, ("starts", "gx"), "gy", None),
        P(None, ("starts", "gx"), "gy", None),
        P("gx", "gy", None),
        P("starts", "gy", None),
    )
    return jax.shard_map(
        on_device,
        mesh=mesh,
        in_specs=placed,
        out_specs=(P(None, ("starts", "gx"), "gy", None), P("starts", "gy", None), P("starts")),
        check_vma=False,
    )
```

```python
import math

import jax
import jax.numpy as jnp
from jax import lax
from jax.sharding import PartitionSpec as P

COUPLING = 1.0
STEP_SIZE = 0.2


def axis_sum(value, axis):
    count = lax.axis_size(axis)
    if count & (count - 1):
        return lax.psum(value, axis)
    step = 1
    while step < count:
        pairs = [(i, i ^ step) for i in range(count)]
        value = value + lax.ppermute(value, axis, pairs)
        step *= 2
    return value


def gx_total(value):
    count = lax.axis_size("gx")
    if count > 8 or count % 2:
        return axis_sum(value, "gx")
    pair = value + lax.ppermute(value, "gx", [(i, i ^ 1) for i in range(count)])
    groups = count // 2
    if groups == 1:
        return pair
    fetched = [pair] + [
        lax.ppermute(pair, "gx", [(i, i ^ (2 * k)) for i in range(count)])
        for k in range(1, groups)
    ]
    stacked = jnp.stack(fetched)
    mine = lax.axis_index("gx") // 2
    total = lax.dynamic_index_in_dim(stacked, mine, keepdims=False)
    for j in range(1, groups):
        total = total + lax.dynamic_index_in_dim(stacked, mine ^ j, keepdims=False)
    return total


def y_extended(block):
    ny = lax.axis_size("gy")
    iy = lax.axis_index("gy")
    Y = block.shape[2]
    if ny == 2:
        strip = jnp.where(iy == 0, block[:, :, Y - 1:], block[:, :, :1])
        other = lax.ppermute(strip, "gy", [(0, 1), (1, 0)])
        zero = jnp.zeros_like(other)
        below = jnp.where(iy == 1, other, zero)
        above = jnp.where(iy == 0, other, zero)
    else:
        below = lax.ppermute(block[:, :, Y - 1:], "gy", [(j, j + 1) for j in range(ny - 1)])
        above = lax.ppermute(block[:, :, :1], "gy", [(j + 1, j) for j in range(ny - 1)])
    return jnp.concatenate([below, block, above], axis=2)


def coefficients(psi, trap, control, profile):
    real_part = psi[0]
    imag_part = psi[1]
    fine_control = jnp.repeat(control, 2, axis=0)
    potential = trap + profile[:, None, None] * fine_control[None, :, :]
    weight = potential + 2.0 * COUPLING * (real_part * real_part + imag_part * imag_part)
    mix_a = COUPLING * (real_part * real_part - imag_part * imag_part)
    mix_b = 2.0 * COUPLING * real_part * imag_part
    return (weight, mix_a, mix_b)


def apply_coef(lapl, field, coef):
    weight, mix_a, mix_b = coef
    real_part = field[0]
    imag_part = field[1]
    upper = -0.5 * lapl[0] + (weight + mix_a) * real_part + mix_b * imag_part
    lower = -0.5 * lapl[1] + mix_b * real_part + (weight - mix_a) * imag_part
    return jnp.stack([-lower, upper])


def operator(tall, x_low, x_high, coef):
    field = tall[:, :, 1:-1]
    x_padded = jnp.concatenate([x_low, field, x_high], axis=1)
    z_padded = jnp.pad(field, ((0, 0), (0, 0), (0, 0), (1, 1)))
    total = x_padded[:, 2:] + x_padded[:, :-2]
    total = total + tall[:, :, 2:] + tall[:, :, :-2]
    total = total + z_padded[:, :, :, 2:] + z_padded[:, :, :, :-2]
    lapl = total - 6.0 * field
    return apply_coef(lapl, field, coef)


def cut(coef, lo, hi):
    return tuple(c[lo:hi] for c in coef)


def across(plane):
    return jnp.stack([0.5 * plane[1], -0.5 * plane[0]])


def with_partner_row(block, row):
    iy = lax.axis_index("gy")
    zero = jnp.zeros_like(row)
    below = jnp.where(iy == 1, row, zero)
    above = jnp.where(iy == 0, row, zero)
    return jnp.concatenate([below, block, above], axis=2)


def edge_rows(block, offset=0):
    iy = lax.axis_index("gy")
    Y = block.shape[2]
    start = (1 - iy) * (Y - 1 - offset) + iy * offset
    return lax.dynamic_slice_in_dim(block, start, 1, axis=2)


def partner_coef(coef):
    rows = jnp.stack([edge_rows(c[:, None])[:, 0] for c in coef])
    got = lax.ppermute(rows, "gy", [(0, 1), (1, 0)])
    return tuple(got[k] for k in range(len(coef)))


def stage_pair(stage, base, base_low, base_high, coef, weight, tall=None, ahead=None):
    nx = lax.axis_size("gx")
    ix = lax.axis_index("gx")
    iy = lax.axis_index("gy")
    X = stage.shape[1]
    up = [(i, i + 1) for i in range(nx - 1)]
    down = [(i + 1, i) for i in range(nx - 1)]
    if tall is None:
        tall = y_extended(stage)
    zero_plane = jnp.zeros_like(stage[:, :1])
    part_top = operator(tall[:, X - 1:], stage[:, X - 2:X - 1], zero_plane, cut(coef, X - 1, X))
    part_bottom = operator(tall[:, :1], zero_plane, stage[:, 1:2], cut(coef, 0, 1))
    from_low = lax.ppermute(jnp.concatenate([stage[:, X - 1:], part_top]), "gx", up)
    from_high = lax.ppermute(jnp.concatenate([stage[:, :1], part_bottom]), "gx", down)
    stage_low, part_low = from_low[:2], from_low[2:]
    stage_high, part_high = from_high[:2], from_high[2:]
    if base_low is None:
        base_low, base_high = stage_low, stage_high
    section = operator(tall, stage_low, stage_high, coef)
    section_low = part_low + across(stage[:, :1])
    section_high = part_high + across(stage[:, X - 1:])
    nxt = base + weight * section
    nxt_low = jnp.where(ix > 0, base_low + weight * section_low, 0.0)
    nxt_high = jnp.where(ix < nx - 1, base_high + weight * section_high, 0.0)
    if ahead is None:
        section_next = operator(y_extended(nxt), nxt_low, nxt_high, coef)
        return section, section_next, base_low, base_high, None
    next_weight, coef_partner = ahead
    mine = edge_rows(nxt)
    pack = jnp.concatenate(
        [mine, edge_rows(nxt, 1), edge_rows(nxt_low), edge_rows(nxt_high)], axis=1
    )
    got = lax.ppermute(pack, "gy", [(0, 1), (1, 0)])
    their, their_inner = got[:, :X], got[:, X:2 * X]
    their_low, their_high = got[:, 2 * X:2 * X + 1], got[:, 2 * X + 1:2 * X + 2]
    section_next = operator(with_partner_row(nxt, their), nxt_low, nxt_high, coef)
    slab = jnp.where(
        iy == 0,
        jnp.concatenate([mine, their, their_inner], axis=2),
        jnp.concatenate([their_inner, their, mine], axis=2),
    )
    their_section = operator(slab, their_low, their_high, coef_partner)
    their_base = jnp.where(iy == 1, tall[:, :, :1], tall[:, :, -1:])
    their_next = their_base + next_weight * their_section
    return section, section_next, base_low, base_high, their_next


def rk_step(field, coef):
    fast = lax.axis_size("gy") == 2 and field.shape[2] >= 3
    ahead = (0.5 * STEP_SIZE, partner_coef(coef)) if fast else None
    section_one, section_two, low, high, their_three = stage_pair(
        field, field, None, None, coef, 0.5 * STEP_SIZE, ahead=ahead
    )
    stage_three = field + 0.5 * STEP_SIZE * section_two
    tall_three = with_partner_row(stage_three, their_three) if fast else None
    section_three, section_four, _, _, _ = stage_pair(
        stage_three, field, low, high, coef, STEP_SIZE, tall=tall_three
    )
    return field + STEP_SIZE / 6.0 * (
        section_one + 2.0 * section_two + 2.0 * section_three + section_four
    )


def row_terms(field, psi, profile):
    intersection = field[0] * psi[1] - field[1] * psi[0]
    summed = jnp.sum(intersection * profile[:, None, None], axis=0)
    return summed.reshape(summed.shape[0] // 2, 2, summed.shape[1]).sum(axis=1)


def on_device(chi_final, psi_late, psi_early, trap, controls):
    planes = chi_final.shape[1]
    width_y = chi_final.shape[2]
    depth = chi_final.shape[3]
    total_x = planes * lax.axis_size("gx")
    total_y = width_y * lax.axis_size("gy")
    first = lax.axis_index("gx") * planes
    x_index = (first + jnp.arange(planes, dtype=jnp.int32)).astype(jnp.float32)
    profile = 1.0 + 0.5 * jnp.cos(2.0 * math.pi * x_index / float(total_x))
    coef_late = coefficients(psi_late, trap, controls[1], profile)
    coef_early = coefficients(psi_early, trap, controls[0], profile)
    chi_late = rk_step(chi_final, coef_late)
    chi_start = rk_step(chi_late, coef_early)
    rows_late = row_terms(chi_late, psi_late, profile)
    rows_early = row_terms(chi_start, psi_early, profile)
    local_sq = axis_sum(jnp.sum(chi_start * chi_start), "gy")
    extra = jnp.zeros((1, rows_early.shape[1]), jnp.float32).at[0, 0].set(local_sq)
    packed = gx_total(jnp.concatenate([rows_early, rows_late, extra], axis=0))
    squares = packed[-1, 0]
    half = rows_early.shape[0]
    rows_sum = jnp.stack([packed[:half], packed[half:2 * half]])
    power = squares / float(total_x * total_y * depth)
    grad_rows = rows_sum / jnp.sqrt(float(total_x) * (power + 1e-06))
    return (chi_start, grad_rows, jnp.reshape(power, (1,)))


def solution(mesh):
    placed = (
        P(None, ("starts", "gx"), "gy", None),
        P(None, ("starts", "gx"), "gy", None),
        P(None, ("starts", "gx"), "gy", None),
        P("gx", "gy", None),
        P("starts", "gy", None),
    )
    return jax.shard_map(
        on_device,
        mesh=mesh,
        in_specs=placed,
        out_specs=(P(None, ("starts", "gx"), "gy", None), P("starts", "gy", None), P("starts")),
        check_vma=False,
    )
```

```python
import math

import jax
import jax.numpy as jnp
from jax import lax
from jax.sharding import PartitionSpec as P

COUPLING = 1.0
STEP_SIZE = 0.2


def axis_sum(value, axis):
    count = lax.axis_size(axis)
    if count & (count - 1):
        return lax.psum(value, axis)
    step = 1
    while step < count:
        pairs = [(i, i ^ step) for i in range(count)]
        value = value + lax.ppermute(value, axis, pairs)
        step *= 2
    return value


def gx_total(value):
    count = lax.axis_size("gx")
    if count > 8 or count % 2:
        return axis_sum(value, "gx")
    pair = value + lax.ppermute(value, "gx", [(i, i ^ 1) for i in range(count)])
    groups = count // 2
    if groups == 1:
        return pair
    fetched = [pair] + [
        lax.ppermute(pair, "gx", [(i, i ^ (2 * k)) for i in range(count)])
        for k in range(1, groups)
    ]
    stacked = jnp.stack(fetched)
    mine = lax.axis_index("gx") // 2
    total = lax.dynamic_index_in_dim(stacked, mine, keepdims=False)
    for j in range(1, groups):
        total = total + lax.dynamic_index_in_dim(stacked, mine ^ j, keepdims=False)
    return total


def y_extended(block):
    ny = lax.axis_size("gy")
    iy = lax.axis_index("gy")
    Y = block.shape[2]
    if ny == 2:
        strip = lax.dynamic_slice_in_dim(block, (1 - iy) * (Y - 1), 1, axis=2)
        other = lax.ppermute(strip, "gy", [(0, 1), (1, 0)])
        zero = jnp.zeros_like(other)
        below = jnp.where(iy == 1, other, zero)
        above = jnp.where(iy == 0, other, zero)
    else:
        below = lax.ppermute(block[:, :, Y - 1:], "gy", [(j, j + 1) for j in range(ny - 1)])
        above = lax.ppermute(block[:, :, :1], "gy", [(j + 1, j) for j in range(ny - 1)])
    return jnp.concatenate([below, block, above], axis=2)


def coefficients(psi, trap, control, profile):
    real_part = psi[0]
    imag_part = psi[1]
    fine_control = jnp.repeat(control, 2, axis=0)
    potential = trap + profile[:, None, None] * fine_control[None, :, :]
    weight = potential + 2.0 * COUPLING * (real_part * real_part + imag_part * imag_part)
    mix_a = COUPLING * (real_part * real_part - imag_part * imag_part)
    mix_b = 2.0 * COUPLING * real_part * imag_part
    return (weight, mix_a, mix_b)


def apply_coef(lapl, field, coef):
    weight, mix_a, mix_b = coef
    real_part = field[0]
    imag_part = field[1]
    upper = -0.5 * lapl[0] + (weight + mix_a) * real_part + mix_b * imag_part
    lower = -0.5 * lapl[1] + mix_b * real_part + (weight - mix_a) * imag_part
    return jnp.stack([-lower, upper])


def operator(tall, x_low, x_high, coef):
    field = tall[:, :, 1:-1]
    x_padded = jnp.concatenate([x_low, field, x_high], axis=1)
    z_padded = jnp.pad(field, ((0, 0), (0, 0), (0, 0), (1, 1)))
    total = x_padded[:, 2:] + x_padded[:, :-2]
    total = total + tall[:, :, 2:] + tall[:, :, :-2]
    total = total + z_padded[:, :, :, 2:] + z_padded[:, :, :, :-2]
    lapl = total - 6.0 * field
    return apply_coef(lapl, field, coef)


def cut(coef, lo, hi):
    return tuple(c[lo:hi] for c in coef)


def across(plane):
    return jnp.stack([0.5 * plane[1], -0.5 * plane[0]])


def with_partner_row(block, row):
    iy = lax.axis_index("gy")
    zero = jnp.zeros_like(row)
    below = jnp.where(iy == 1, row, zero)
    above = jnp.where(iy == 0, row, zero)
    return jnp.concatenate([below, block, above], axis=2)


def edge_rows(block, offset=0):
    iy = lax.axis_index("gy")
    Y = block.shape[2]
    start = (1 - iy) * (Y - 1 - offset) + iy * offset
    return lax.dynamic_slice_in_dim(block, start, 1, axis=2)


def partner_coef(coef):
    rows = jnp.stack([edge_rows(c[:, None])[:, 0] for c in coef])
    got = lax.ppermute(rows, "gy", [(0, 1), (1, 0)])
    return tuple(got[k] for k in range(len(coef)))


def stage_pair(stage, base, base_low, base_high, coef, weight, tall=None, ahead=None):
    nx = lax.axis_size("gx")
    ix = lax.axis_index("gx")
    iy = lax.axis_index("gy")
    X = stage.shape[1]
    up = [(i, i + 1) for i in range(nx - 1)]
    down = [(i + 1, i) for i in range(nx - 1)]
    if tall is None:
        tall = y_extended(stage)
    zero_plane = jnp.zeros_like(stage[:, :1])
    part_top = operator(tall[:, X - 1:], stage[:, X - 2:X - 1], zero_plane, cut(coef, X - 1, X))
    part_bottom = operator(tall[:, :1], zero_plane, stage[:, 1:2], cut(coef, 0, 1))
    from_low = lax.ppermute(jnp.concatenate([stage[:, X - 1:], part_top]), "gx", up)
    from_high = lax.ppermute(jnp.concatenate([stage[:, :1], part_bottom]), "gx", down)
    stage_low, part_low = from_low[:2], from_low[2:]
    stage_high, part_high = from_high[:2], from_high[2:]
    if base_low is None:
        base_low, base_high = stage_low, stage_high
    section = operator(tall, stage_low, stage_high, coef)
    section_low = part_low + across(stage[:, :1])
    section_high = part_high + across(stage[:, X - 1:])
    nxt = base + weight * section
    nxt_low = jnp.where(ix > 0, base_low + weight * section_low, 0.0)
    nxt_high = jnp.where(ix < nx - 1, base_high + weight * section_high, 0.0)
    if ahead is None:
        section_next = operator(y_extended(nxt), nxt_low, nxt_high, coef)
        return section, section_next, base_low, base_high, None
    next_weight, coef_partner = ahead
    mine = edge_rows(nxt)
    pack = jnp.concatenate(
        [mine, edge_rows(nxt, 1), edge_rows(nxt_low), edge_rows(nxt_high)], axis=1
    )
    got = lax.ppermute(pack, "gy", [(0, 1), (1, 0)])
    their, their_inner = got[:, :X], got[:, X:2 * X]
    their_low, their_high = got[:, 2 * X:2 * X + 1], got[:, 2 * X + 1:2 * X + 2]
    section_next = operator(with_partner_row(nxt, their), nxt_low, nxt_high, coef)
    slab = jnp.where(
        iy == 0,
        jnp.concatenate([mine, their, their_inner], axis=2),
        jnp.concatenate([their_inner, their, mine], axis=2),
    )
    their_section = operator(slab, their_low, their_high, coef_partner)
    their_base = jnp.where(iy == 1, tall[:, :, :1], tall[:, :, -1:])
    their_next = their_base + next_weight * their_section
    return section, section_next, base_low, base_high, their_next


def rk_step(field, coef):
    fast = lax.axis_size("gy") == 2 and field.shape[2] >= 3
    ahead = (0.5 * STEP_SIZE, partner_coef(coef)) if fast else None
    section_one, section_two, low, high, their_three = stage_pair(
        field, field, None, None, coef, 0.5 * STEP_SIZE, ahead=ahead
    )
    stage_three = field + 0.5 * STEP_SIZE * section_two
    tall_three = with_partner_row(stage_three, their_three) if fast else None
    section_three, section_four, _, _, _ = stage_pair(
        stage_three, field, low, high, coef, STEP_SIZE, tall=tall_three
    )
    return field + STEP_SIZE / 6.0 * (
        section_one + 2.0 * section_two + 2.0 * section_three + section_four
    )


def row_terms(field, psi, profile):
    intersection = field[0] * psi[1] - field[1] * psi[0]
    summed = jnp.sum(intersection * profile[:, None, None], axis=0)
    return summed.reshape(summed.shape[0] // 2, 2, summed.shape[1]).sum(axis=1)


def on_device(chi_final, psi_late, psi_early, trap, controls):
    planes = chi_final.shape[1]
    width_y = chi_final.shape[2]
    depth = chi_final.shape[3]
    total_x = planes * lax.axis_size("gx")
    total_y = width_y * lax.axis_size("gy")
    first = lax.axis_index("gx") * planes
    x_index = (first + jnp.arange(planes, dtype=jnp.int32)).astype(jnp.float32)
    profile = 1.0 + 0.5 * jnp.cos(2.0 * math.pi * x_index / float(total_x))
    coef_late = coefficients(psi_late, trap, controls[1], profile)
    coef_early = coefficients(psi_early, trap, controls[0], profile)
    chi_late = rk_step(chi_final, coef_late)
    chi_start = rk_step(chi_late, coef_early)
    rows_late = row_terms(chi_late, psi_late, profile)
    rows_early = row_terms(chi_start, psi_early, profile)
    local_sq = axis_sum(jnp.sum(chi_start * chi_start), "gy")
    extra = jnp.zeros((1, rows_early.shape[1]), jnp.float32).at[0, 0].set(local_sq)
    packed = gx_total(jnp.concatenate([rows_early, rows_late, extra], axis=0))
    squares = packed[-1, 0]
    half = rows_early.shape[0]
    rows_sum = packed[:2 * half].reshape(2, half, packed.shape[1])
    power = squares / float(total_x * total_y * depth)
    grad_rows = rows_sum / jnp.sqrt(float(total_x) * (power + 1e-06))
    return (chi_start, grad_rows, jnp.reshape(power, (1,)))


def solution(mesh):
    placed = (
        P(None, ("starts", "gx"), "gy", None),
        P(None, ("starts", "gx"), "gy", None),
        P(None, ("starts", "gx"), "gy", None),
        P("gx", "gy", None),
        P("starts", "gy", None),
    )
    return jax.shard_map(
        on_device,
        mesh=mesh,
        in_specs=placed,
        out_specs=(P(None, ("starts", "gx"), "gy", None), P("starts", "gy", None), P("starts")),
        check_vma=False,
    )
```

```python
import math

import jax
import jax.numpy as jnp
from jax import lax
from jax.sharding import PartitionSpec as P

COUPLING = 1.0
STEP_SIZE = 0.2


def axis_sum(value, axis):
    count = lax.axis_size(axis)
    if count & (count - 1):
        return lax.psum(value, axis)
    step = 1
    while step < count:
        pairs = [(i, i ^ step) for i in range(count)]
        value = value + lax.ppermute(value, axis, pairs)
        step *= 2
    return value


def gx_total(value):
    count = lax.axis_size("gx")
    if count > 8 or count % 2:
        return axis_sum(value, "gx")
    pair = value + lax.ppermute(value, "gx", [(i, i ^ 1) for i in range(count)])
    groups = count // 2
    if groups == 1:
        return pair
    fetched = [pair] + [
        lax.ppermute(pair, "gx", [(i, i ^ (2 * k)) for i in range(count)])
        for k in range(1, groups)
    ]
    stacked = jnp.stack(fetched)
    mine = lax.axis_index("gx") // 2
    total = lax.dynamic_index_in_dim(stacked, mine, keepdims=False)
    for j in range(1, groups):
        total = total + lax.dynamic_index_in_dim(stacked, mine ^ j, keepdims=False)
    return total


def y_extended(block):
    ny = lax.axis_size("gy")
    iy = lax.axis_index("gy")
    Y = block.shape[2]
    if ny == 2:
        strip = lax.dynamic_slice_in_dim(block, (1 - iy) * (Y - 1), 1, axis=2)
        other = lax.ppermute(strip, "gy", [(0, 1), (1, 0)])
        zero = jnp.zeros_like(other)
        below = jnp.where(iy == 1, other, zero)
        above = jnp.where(iy == 0, other, zero)
    else:
        below = lax.ppermute(block[:, :, Y - 1:], "gy", [(j, j + 1) for j in range(ny - 1)])
        above = lax.ppermute(block[:, :, :1], "gy", [(j + 1, j) for j in range(ny - 1)])
    return jnp.concatenate([below, block, above], axis=2)


def coefficients(psi, trap, control, profile):
    real_part = psi[0]
    imag_part = psi[1]
    fine_control = jnp.repeat(control, 2, axis=0)
    potential = trap + profile[:, None, None] * fine_control[None, :, :]
    weight = potential + 2.0 * COUPLING * (real_part * real_part + imag_part * imag_part)
    mix_a = COUPLING * (real_part * real_part - imag_part * imag_part)
    mix_b = 2.0 * COUPLING * real_part * imag_part
    return (weight, mix_a, mix_b)


def apply_coef(lapl, field, coef):
    weight, mix_a, mix_b = coef
    real_part = field[0]
    imag_part = field[1]
    upper = -0.5 * lapl[0] + (weight + mix_a) * real_part + mix_b * imag_part
    lower = -0.5 * lapl[1] + mix_b * real_part + (weight - mix_a) * imag_part
    return jnp.stack([-lower, upper])


def operator(tall, x_low, x_high, coef):
    field = tall[:, :, 1:-1]
    x_padded = jnp.concatenate([x_low, field, x_high], axis=1)
    z_padded = jnp.pad(field, ((0, 0), (0, 0), (0, 0), (1, 1)))
    total = x_padded[:, 2:] + x_padded[:, :-2]
    total = total + tall[:, :, 2:] + tall[:, :, :-2]
    total = total + z_padded[:, :, :, 2:] + z_padded[:, :, :, :-2]
    lapl = total - 6.0 * field
    return apply_coef(lapl, field, coef)


def cut(coef, lo, hi):
    return tuple(c[lo:hi] for c in coef)


def across(plane):
    return jnp.stack([0.5 * plane[1], -0.5 * plane[0]])


def with_partner_row(block, row):
    iy = lax.axis_index("gy")
    zero = jnp.zeros_like(row)
    below = jnp.where(iy == 1, row, zero)
    above = jnp.where(iy == 0, row, zero)
    return jnp.concatenate([below, block, above], axis=2)


def edge_rows(block, offset=0):
    iy = lax.axis_index("gy")
    Y = block.shape[2]
    start = (1 - iy) * (Y - 1 - offset) + iy * offset
    return lax.dynamic_slice_in_dim(block, start, 1, axis=2)


def partner_coef(coef):
    rows = jnp.stack([edge_rows(c[:, None])[:, 0] for c in coef])
    got = lax.ppermute(rows, "gy", [(0, 1), (1, 0)])
    return tuple(got[k] for k in range(len(coef)))


def stage_pair(stage, base, base_low, base_high, coef, weight, tall=None, ahead=None):
    nx = lax.axis_size("gx")
    ix = lax.axis_index("gx")
    iy = lax.axis_index("gy")
    X = stage.shape[1]
    up = [(i, i + 1) for i in range(nx - 1)]
    down = [(i + 1, i) for i in range(nx - 1)]
    if tall is None:
        tall = y_extended(stage)
    zero_plane = jnp.zeros_like(stage[:, :1])
    part_top = operator(tall[:, X - 1:], stage[:, X - 2:X - 1], zero_plane, cut(coef, X - 1, X))
    part_bottom = operator(tall[:, :1], zero_plane, stage[:, 1:2], cut(coef, 0, 1))
    from_low = lax.ppermute(jnp.concatenate([stage[:, X - 1:], part_top]), "gx", up)
    from_high = lax.ppermute(jnp.concatenate([stage[:, :1], part_bottom]), "gx", down)
    stage_low, part_low = from_low[:2], from_low[2:]
    stage_high, part_high = from_high[:2], from_high[2:]
    if base_low is None:
        base_low, base_high = stage_low, stage_high
    section = operator(tall, stage_low, stage_high, coef)
    section_low = part_low + across(stage[:, :1])
    section_high = part_high + across(stage[:, X - 1:])
    nxt = base + weight * section
    nxt_low = jnp.where(ix > 0, base_low + weight * section_low, 0.0)
    nxt_high = jnp.where(ix < nx - 1, base_high + weight * section_high, 0.0)
    if ahead is None:
        section_next = operator(y_extended(nxt), nxt_low, nxt_high, coef)
        return section, section_next, base_low, base_high, None
    next_weight, coef_partner = ahead
    mine = edge_rows(nxt)
    pack = jnp.concatenate(
        [mine, edge_rows(nxt, 1), edge_rows(nxt_low), edge_rows(nxt_high)], axis=1
    )
    got = lax.ppermute(pack, "gy", [(0, 1), (1, 0)])
    their, their_inner = got[:, :X], got[:, X:2 * X]
    their_low, their_high = got[:, 2 * X:2 * X + 1], got[:, 2 * X + 1:2 * X + 2]
    section_next = operator(with_partner_row(nxt, their), nxt_low, nxt_high, coef)
    slab = jnp.where(
        iy == 0,
        jnp.concatenate([mine, their, their_inner], axis=2),
        jnp.concatenate([their_inner, their, mine], axis=2),
    )
    their_section = operator(slab, their_low, their_high, coef_partner)
    their_base = jnp.where(iy == 1, tall[:, :, :1], tall[:, :, -1:])
    their_next = their_base + next_weight * their_section
    return section, section_next, base_low, base_high, their_next


def rk_step(field, coef):
    fast = lax.axis_size("gy") == 2 and field.shape[2] >= 3
    ahead = (0.5 * STEP_SIZE, partner_coef(coef)) if fast else None
    section_one, section_two, low, high, their_three = stage_pair(
        field, field, None, None, coef, 0.5 * STEP_SIZE, ahead=ahead
    )
    stage_three = field + 0.5 * STEP_SIZE * section_two
    tall_three = with_partner_row(stage_three, their_three) if fast else None
    section_three, section_four, _, _, _ = stage_pair(
        stage_three, field, low, high, coef, STEP_SIZE, tall=tall_three
    )
    return field + STEP_SIZE / 6.0 * (
        section_one + 2.0 * section_two + 2.0 * section_three + section_four
    )


def row_terms(field, psi, profile):
    intersection = field[0] * psi[1] - field[1] * psi[0]
    summed = jnp.sum(intersection * profile[:, None, None], axis=0)
    return summed.reshape(summed.shape[0] // 2, 2, summed.shape[1]).sum(axis=1)


def on_device(chi_final, psi_late, psi_early, trap, controls):
    planes = chi_final.shape[1]
    width_y = chi_final.shape[2]
    depth = chi_final.shape[3]
    total_x = planes * lax.axis_size("gx")
    total_y = width_y * lax.axis_size("gy")
    first = lax.axis_index("gx") * planes
    x_index = (first + jnp.arange(planes, dtype=jnp.int32)).astype(jnp.float32)
    profile = 1.0 + 0.5 * jnp.cos(2.0 * math.pi * x_index / float(total_x))
    coef_late = coefficients(psi_late, trap, controls[1], profile)
    coef_early = coefficients(psi_early, trap, controls[0], profile)
    chi_late = rk_step(chi_final, coef_late)
    chi_start = rk_step(chi_late, coef_early)
    rows_late = row_terms(chi_late, psi_late, profile)
    rows_early = row_terms(chi_start, psi_early, profile)
    local_sq = axis_sum(jnp.sum(chi_start * chi_start), "gy")
    extra = jnp.zeros((1, rows_early.shape[1]), jnp.float32).at[0, 0].set(local_sq)
    packed = gx_total(jnp.concatenate([rows_early, rows_late, extra], axis=0))
    half = rows_early.shape[0]
    rows_sum = packed[:2 * half].reshape(2, half, packed.shape[1])
    power = packed[-1, 0] / float(total_x * total_y * depth)
    scale = jnp.sum(packed[-1]) / float(total_x * total_y * depth)
    grad_rows = rows_sum / jnp.sqrt(float(total_x) * (scale + 1e-06))
    return (chi_start, grad_rows, jnp.reshape(power, (1,)))


def solution(mesh):
    placed = (
        P(None, ("starts", "gx"), "gy", None),
        P(None, ("starts", "gx"), "gy", None),
        P(None, ("starts", "gx"), "gy", None),
        P("gx", "gy", None),
        P("starts", "gy", None),
    )
    return jax.shard_map(
        on_device,
        mesh=mesh,
        in_specs=placed,
        out_specs=(P(None, ("starts", "gx"), "gy", None), P("starts", "gy", None), P("starts")),
        check_vma=False,
    )
```

```python
import math

import jax
import jax.numpy as jnp
from jax import lax
from jax.sharding import PartitionSpec as P

COUPLING = 1.0
STEP_SIZE = 0.2


def axis_sum(value, axis):
    count = lax.axis_size(axis)
    if count & (count - 1):
        return lax.psum(value, axis)
    step = 1
    while step < count:
        pairs = [(i, i ^ step) for i in range(count)]
        value = value + lax.ppermute(value, axis, pairs)
        step *= 2
    return value


def gx_total(value):
    count = lax.axis_size("gx")
    if count > 4 or count % 2:
        return axis_sum(value, "gx")
    pair = value + lax.ppermute(value, "gx", [(i, i ^ 1) for i in range(count)])
    groups = count // 2
    if groups == 1:
        return pair
    fetched = [pair] + [
        lax.ppermute(pair, "gx", [(i, i ^ (2 * k)) for i in range(count)])
        for k in range(1, groups)
    ]
    stacked = jnp.stack(fetched)
    mine = lax.axis_index("gx") // 2
    total = lax.dynamic_index_in_dim(stacked, mine, keepdims=False)
    for j in range(1, groups):
        total = total + lax.dynamic_index_in_dim(stacked, mine ^ j, keepdims=False)
    return total


def y_extended(block):
    ny = lax.axis_size("gy")
    iy = lax.axis_index("gy")
    Y = block.shape[2]
    if ny == 2:
        strip = lax.dynamic_slice_in_dim(block, (1 - iy) * (Y - 1), 1, axis=2)
        other = lax.ppermute(strip, "gy", [(0, 1), (1, 0)])
        zero = jnp.zeros_like(other)
        below = jnp.where(iy == 1, other, zero)
        above = jnp.where(iy == 0, other, zero)
    else:
        below = lax.ppermute(block[:, :, Y - 1:], "gy", [(j, j + 1) for j in range(ny - 1)])
        above = lax.ppermute(block[:, :, :1], "gy", [(j + 1, j) for j in range(ny - 1)])
    return jnp.concatenate([below, block, above], axis=2)


def coefficients(psi, trap, control, profile):
    real_part = psi[0]
    imag_part = psi[1]
    fine_control = jnp.repeat(control, 2, axis=0)
    potential = trap + profile[:, None, None] * fine_control[None, :, :]
    weight = potential + 2.0 * COUPLING * (real_part * real_part + imag_part * imag_part)
    mix_a = COUPLING * (real_part * real_part - imag_part * imag_part)
    mix_b = 2.0 * COUPLING * real_part * imag_part
    return (weight, mix_a, mix_b)


def apply_coef(lapl, field, coef):
    weight, mix_a, mix_b = coef
    real_part = field[0]
    imag_part = field[1]
    upper = -0.5 * lapl[0] + (weight + mix_a) * real_part + mix_b * imag_part
    lower = -0.5 * lapl[1] + mix_b * real_part + (weight - mix_a) * imag_part
    return jnp.stack([-lower, upper])


def operator(tall, x_low, x_high, coef):
    field = tall[:, :, 1:-1]
    x_padded = jnp.concatenate([x_low, field, x_high], axis=1)
    z_padded = jnp.pad(field, ((0, 0), (0, 0), (0, 0), (1, 1)))
    total = x_padded[:, 2:] + x_padded[:, :-2]
    total = total + tall[:, :, 2:] + tall[:, :, :-2]
    total = total + z_padded[:, :, :, 2:] + z_padded[:, :, :, :-2]
    lapl = total - 6.0 * field
    return apply_coef(lapl, field, coef)


def cut(coef, lo, hi):
    return tuple(c[lo:hi] for c in coef)


def across(plane):
    return jnp.stack([0.5 * plane[1], -0.5 * plane[0]])


def with_partner_row(block, row):
    iy = lax.axis_index("gy")
    zero = jnp.zeros_like(row)
    below = jnp.where(iy == 1, row, zero)
    above = jnp.where(iy == 0, row, zero)
    return jnp.concatenate([below, block, above], axis=2)


def edge_rows(block, offset=0):
    iy = lax.axis_index("gy")
    Y = block.shape[2]
    start = (1 - iy) * (Y - 1 - offset) + iy * offset
    return lax.dynamic_slice_in_dim(block, start, 1, axis=2)


def partner_coef(coef):
    rows = jnp.stack([edge_rows(c[:, None])[:, 0] for c in coef])
    got = lax.ppermute(rows, "gy", [(0, 1), (1, 0)])
    return tuple(got[k] for k in range(len(coef)))


def stage_pair(stage, base, base_low, base_high, coef, weight, tall=None, ahead=None):
    nx = lax.axis_size("gx")
    ix = lax.axis_index("gx")
    iy = lax.axis_index("gy")
    X = stage.shape[1]
    up = [(i, i + 1) for i in range(nx - 1)]
    down = [(i + 1, i) for i in range(nx - 1)]
    if tall is None:
        tall = y_extended(stage)
    zero_plane = jnp.zeros_like(stage[:, :1])
    part_top = operator(tall[:, X - 1:], stage[:, X - 2:X - 1], zero_plane, cut(coef, X - 1, X))
    part_bottom = operator(tall[:, :1], zero_plane, stage[:, 1:2], cut(coef, 0, 1))
    from_low = lax.ppermute(jnp.concatenate([stage[:, X - 1:], part_top]), "gx", up)
    from_high = lax.ppermute(jnp.concatenate([stage[:, :1], part_bottom]), "gx", down)
    stage_low, part_low = from_low[:2], from_low[2:]
    stage_high, part_high = from_high[:2], from_high[2:]
    if base_low is None:
        base_low, base_high = stage_low, stage_high
    section = operator(tall, stage_low, stage_high, coef)
    section_low = part_low + across(stage[:, :1])
    section_high = part_high + across(stage[:, X - 1:])
    nxt = base + weight * section
    nxt_low = jnp.where(ix > 0, base_low + weight * section_low, 0.0)
    nxt_high = jnp.where(ix < nx - 1, base_high + weight * section_high, 0.0)
    if ahead is None:
        section_next = operator(y_extended(nxt), nxt_low, nxt_high, coef)
        return section, section_next, base_low, base_high, None
    next_weight, coef_partner = ahead
    mine = edge_rows(nxt)
    pack = jnp.concatenate(
        [mine, edge_rows(nxt, 1), edge_rows(nxt_low), edge_rows(nxt_high)], axis=1
    )
    got = lax.ppermute(pack, "gy", [(0, 1), (1, 0)])
    their, their_inner = got[:, :X], got[:, X:2 * X]
    their_low, their_high = got[:, 2 * X:2 * X + 1], got[:, 2 * X + 1:2 * X + 2]
    section_next = operator(with_partner_row(nxt, their), nxt_low, nxt_high, coef)
    slab = jnp.where(
        iy == 0,
        jnp.concatenate([mine, their, their_inner], axis=2),
        jnp.concatenate([their_inner, their, mine], axis=2),
    )
    their_section = operator(slab, their_low, their_high, coef_partner)
    their_base = jnp.where(iy == 1, tall[:, :, :1], tall[:, :, -1:])
    their_next = their_base + next_weight * their_section
    return section, section_next, base_low, base_high, their_next


def rk_step(field, coef):
    fast = lax.axis_size("gy") == 2 and field.shape[2] >= 3
    ahead = (0.5 * STEP_SIZE, partner_coef(coef)) if fast else None
    section_one, section_two, low, high, their_three = stage_pair(
        field, field, None, None, coef, 0.5 * STEP_SIZE, ahead=ahead
    )
    stage_three = field + 0.5 * STEP_SIZE * section_two
    tall_three = with_partner_row(stage_three, their_three) if fast else None
    section_three, section_four, _, _, _ = stage_pair(
        stage_three, field, low, high, coef, STEP_SIZE, tall=tall_three
    )
    return field + STEP_SIZE / 6.0 * (
        section_one + 2.0 * section_two + 2.0 * section_three + section_four
    )


def row_terms(field, psi, profile):
    intersection = field[0] * psi[1] - field[1] * psi[0]
    summed = jnp.sum(intersection * profile[:, None, None], axis=0)
    return summed.reshape(summed.shape[0] // 2, 2, summed.shape[1]).sum(axis=1)


def on_device(chi_final, psi_late, psi_early, trap, controls):
    planes = chi_final.shape[1]
    width_y = chi_final.shape[2]
    depth = chi_final.shape[3]
    total_x = planes * lax.axis_size("gx")
    total_y = width_y * lax.axis_size("gy")
    first = lax.axis_index("gx") * planes
    x_index = (first + jnp.arange(planes, dtype=jnp.int32)).astype(jnp.float32)
    profile = 1.0 + 0.5 * jnp.cos(2.0 * math.pi * x_index / float(total_x))
    coef_late = coefficients(psi_late, trap, controls[1], profile)
    coef_early = coefficients(psi_early, trap, controls[0], profile)
    chi_late = rk_step(chi_final, coef_late)
    chi_start = rk_step(chi_late, coef_early)
    rows_late = row_terms(chi_late, psi_late, profile)
    rows_early = row_terms(chi_start, psi_early, profile)
    local_sq = axis_sum(jnp.sum(chi_start * chi_start), "gy")
    extra = jnp.zeros((1, rows_early.shape[1]), jnp.float32).at[0, 0].set(local_sq)
    packed = gx_total(jnp.concatenate([rows_early, rows_late, extra], axis=0))
    squares = packed[-1, 0]
    half = rows_early.shape[0]
    rows_sum = packed[:2 * half].reshape(2, half, packed.shape[1])
    power = squares / float(total_x * total_y * depth)
    grad_rows = rows_sum / jnp.sqrt(float(total_x) * (power + 1e-06))
    return (chi_start, grad_rows, jnp.reshape(power, (1,)))


def solution(mesh):
    placed = (
        P(None, ("starts", "gx"), "gy", None),
        P(None, ("starts", "gx"), "gy", None),
        P(None, ("starts", "gx"), "gy", None),
        P("gx", "gy", None),
        P("starts", "gy", None),
    )
    return jax.shard_map(
        on_device,
        mesh=mesh,
        in_specs=placed,
        out_specs=(P(None, ("starts", "gx"), "gy", None), P("starts", "gy", None), P("starts")),
        check_vma=False,
    )
```
